32 devices in a mesh: leaf: 8 (over z, x), panel: 4 (over y, core).
Axes of the slice: x: 2, y: 2, z: 4, core: 2. Of those that a mesh axis runs over, the one named last changes fastest.
Arguments:
- upper_rhs: float32 [8, 512, 128], P('leaf'), may hold values from -6 to 6
- upper_panel: float32 [8, 1024, 512], P('leaf', 'panel'), may hold values from -0.25 to 0.25
- upper_inverse: float32 [8, 512, 512], P('leaf'), as said below
- top_index: int32 [8, 1024], P('leaf', 'panel'), may hold values from 0 to 511
- top_solution: float32 [512, 128], P(('leaf', 'panel')), may hold values from -6 to 6
- owner_map: int32 [8], replicated, may hold values from 0 to 7, each once
- parent_list: int32 [256], P(('leaf', 'panel')), may hold values from 0 to 7, as said below
- lower_index: int32 [256, 256], P(('leaf', 'panel')), may hold values from 0 to 511
- lower_panel: float32 [256, 256, 256], P(('leaf', 'panel')), may hold values from -0.5 to 0.5
- lower_rhs: float32 [256, 256, 128], P(('leaf', 'panel')), may hold values from -6 to 6
- lower_inverse: float32 [256, 256, 256], P(('leaf', 'panel')), as said below
Outputs:
- upper_solution: float32 [8, 512, 128], P('leaf', 'panel')
- lower_solution: float32 [256, 256, 128], P(('leaf', 'panel'))
The draws below stay inside these ranges and needn't reach their ends.
Inputs may be any that keep to these rules, and one draw needn't show every extreme that they name: `owner_map`: each leaf index holds exactly one upper supernode. `parent_list`: the 8 lower supernodes of one device have pairwise different parents. `upper_inverse`: lower triangular with a positive diagonal. `lower_inverse`: lower triangular with a positive diagonal.
All inputs are finite; a program needn't handle non-finite values.
Results may differ from the reference program's by a relative error of at most 0.00007.
Values sent between devices are 32-bit elements; how exact they have to be, the bound alone decides.
No kernel may reach another device: no remote copies, remote signals or barrier semaphores. Data moves between devices by JAX's collectives and lax.ppermute only.
A program may use at most 64 MiB of HBM per device.

```python
import jax
import jax.numpy as jnp
from jax import lax

RHS = 128
WU = 512
KU = 1024
WL = 256
KL = 256
LOW_DEV = 8
NU = 8
NTOP = 512
NLOW = 256


def lower_triangle(key, count, width):
    first = jax.random.fold_in(key, 11)
    second = jax.random.fold_in(key, 23)
    spread = jax.random.normal(first, (count, width, width), jnp.float32)
    spread = spread * (0.7 / width ** 0.5)
    diagonal = jax.random.uniform(second, (count, width), jnp.float32, 0.6, 1.4)
    rows = jnp.arange(width)
    below = rows[:, None] > rows[None, :]
    same = rows[:, None] == rows[None, :]
    return jnp.where(below[None], spread, 0.0) + jnp.where(same[None], diagonal[:, :, None], 0.0)


def draw_upper_inverse(key, part):
    return lower_triangle(key, NU, WU).astype(jnp.float32)


def draw_lower_inverse(key, part):
    return lower_triangle(key, NLOW, WL).astype(jnp.float32)


def draw_parent_list(key, part):
    blocks = NLOW // LOW_DEV
    base = jax.random.fold_in(key, 37)
    block_keys = jax.vmap(lambda number: jax.random.fold_in(base, number))(jnp.arange(blocks))
    orders = jax.vmap(lambda single: jax.random.permutation(single, NU))(block_keys)
    return orders[:, :LOW_DEV].reshape(NLOW).astype(jnp.int32)


def set_ends(values, stream_key, smallest, top_value):
    longest = values.shape.index(max(values.shape))
    spots = []
    for shift in (0, 1):
        where = [jax.random.randint(jax.random.fold_in(stream_key, axis), (), 0, length) for axis, length in enumerate(values.shape)]
        where[longest] = (where[longest] + shift) % values.shape[longest]
        spots.append(tuple(where))
    return values.at[spots[0]].set(smallest).at[spots[1]].set(top_value)


def levels(stream_key, extent, pieces, smallest, largest):
    level, own = 1.0, jax.random.fold_in(stream_key, 6)
    for dim, parts in pieces:
        heights = jnp.exp(jax.random.uniform(jax.random.fold_in(own, dim), (parts,), jnp.float32, smallest / len(pieces), largest / len(pieces)))
        level = level * jnp.repeat(heights, extent[dim] // parts).reshape([-1 if axis == dim else 1 for axis in range(len(extent))])
    return level


def scatter_about(stream_key, dims, scale, limit, shards=(), kind=jnp.bfloat16):
    array = jax.random.normal(stream_key, dims, jnp.float32) * scale
    if len(shards) > 0:
        array = levels(stream_key, dims, shards, -0.22, 0.18) * array
    return jnp.clip(array, min=-limit, max=limit).astype(kind)


def setup_inputs(seed: int = 0) -> dict:
    seeds = jax.random.split(jax.random.key(seed), 12)
    return {
        "upper_rhs": scatter_about(seeds[0], (NU, WU, RHS), 1.0, 6.0, ((0, 8),), jnp.float32),
        "upper_panel": scatter_about(seeds[1], (NU, KU, WU), (KU // 2) ** -0.5, 0.25, ((0, 8), (1, 4)), jnp.float32),
        "upper_inverse": draw_upper_inverse(jax.random.fold_in(seeds[11], 71), 0),
        "top_index": set_ends(jax.random.randint(seeds[3], (NU, KU), 0, NTOP), jax.random.fold_in(seeds[3], 1), 0, NTOP - 1).astype(jnp.int32),
        "top_solution": scatter_about(seeds[4], (NTOP, RHS), 1.0, 6.0, ((0, 32),), jnp.float32),
        "owner_map": jax.random.permutation(seeds[5], NU).astype(jnp.int32),
        "parent_list": draw_parent_list(jax.random.fold_in(seeds[11], 71), 0),
        "lower_index": set_ends(jax.random.randint(seeds[7], (NLOW, KL), 0, WU), jax.random.fold_in(seeds[7], 1), 0, WU - 1).astype(jnp.int32),
        "lower_panel": scatter_about(seeds[8], (NLOW, KL, WL), (KL // 2) ** -0.5, 0.5, ((0, 32),), jnp.float32),
        "lower_rhs": scatter_about(seeds[9], (NLOW, WL, RHS), 1.0, 6.0, ((0, 32),), jnp.float32),
        "lower_inverse": draw_lower_inverse(jax.random.fold_in(seeds[11], 71), 0),
    }


def reference(upper_rhs, upper_panel, upper_inverse, top_index, top_solution, owner_map, parent_list, lower_index, lower_panel, lower_rhs, lower_inverse):
    highest = lax.Precision.HIGHEST
    gathered = top_solution[top_index]
    update = jnp.einsum('ukw,ukr->uwr', upper_panel, gathered, precision=highest)
    reduced = upper_rhs - update
    upper_solution = jnp.einsum('ukw,ukr->uwr', upper_inverse, reduced, precision=highest)
    position = owner_map[parent_list]
    parent_rows = upper_solution[position[:, None], lower_index]
    lower_update = jnp.einsum('skw,skr->swr', lower_panel, parent_rows, precision=highest)
    lower_solution = jnp.einsum('skw,skr->swr', lower_inverse, lower_rhs - lower_update, precision=highest)
    return (upper_solution, lower_solution)
```

```python
import jax
import jax.numpy as jnp
from jax import lax
from jax.sharding import PartitionSpec as P


def doubling_gather(block, axes, count):
    bits = count.bit_length() - 1
    if (1 << bits) != count:
        return lax.all_gather(block, axes, axis=0, tiled=True)
    index = lax.axis_index(axes)
    held = block[None]
    for bit in reversed(range(bits)):
        pairs = [(i, i ^ (1 << bit)) for i in range(count)]
        received = lax.ppermute(held, axes, pairs)
        upper = ((index >> bit) & 1) == 1
        held = jnp.where(upper, jnp.concatenate([received, held], 0), jnp.concatenate([held, received], 0))
    shape = held.shape[1:]
    held = held.reshape((2,) * bits + shape)
    held = jnp.transpose(held, tuple(reversed(range(bits))) + tuple(range(bits, bits + len(shape))))
    held = held.reshape((count,) + shape)
    return held.reshape((count * shape[0],) + shape[1:])


def butterfly_sum(value, axis, count):
    bits = count.bit_length() - 1
    if (1 << bits) != count:
        return lax.psum(value, axis)
    for bit in range(bits):
        pairs = [(i, i ^ (1 << bit)) for i in range(count)]
        value = value + lax.ppermute(value, axis, pairs)
    return value


def local(
    upper_rhs,
    upper_panel,
    upper_inverse,
    top_index,
    top_solution,
    owner_map,
    parent_list,
    lower_index,
    lower_panel,
    lower_rhs,
    lower_inverse,
):
    highest = lax.Precision.HIGHEST
    leaves = lax.axis_size("leaf")
    panels = lax.axis_size("panel")
    panel_index = lax.axis_index("panel")
    width_upper = upper_rhs.shape[1]
    share = width_upper // panels
    begin = panel_index * share
    both = ("leaf", "panel")
    top_whole = doubling_gather(top_solution, both, leaves * panels)
    gathered = top_whole[top_index[0]]
    partial_update = jnp.einsum("kw,kr->wr", upper_panel[0], gathered, precision=highest)
    update = butterfly_sum(partial_update, "panel", panels)
    reduced = upper_rhs[0] - update
    full_solution = jnp.einsum("kw,kr->wr", upper_inverse[0], reduced, precision=highest)
    own_rows = lax.dynamic_slice_in_dim(full_solution, begin, share, 0)
    all_upper = doubling_gather(own_rows, both, leaves * panels)
    all_upper = all_upper.reshape(leaves, width_upper, all_upper.shape[-1])
    position = owner_map[parent_list]
    slabs = all_upper[position]
    columns = lax.broadcasted_iota(jnp.int32, lower_index.shape + (width_upper,), 2)
    pick = (lower_index[:, :, None] == columns).astype(jnp.float32)
    parent_rows = jnp.einsum("skj,sjr->skr", pick, slabs, precision=highest)
    lower_update = jnp.einsum("skw,skr->swr", lower_panel, parent_rows, precision=highest)
    lower_solution = jnp.einsum(
        "skw,skr->swr", lower_inverse, lower_rhs - lower_update, precision=highest
    )
    return (own_rows[None], lower_solution)


def solution(mesh):
    placed = (
        P("leaf", None, None),
        P("leaf", "panel", None),
        P("leaf", None, None),
        P("leaf", "panel"),
        P(("leaf", "panel"), None),
        P(),
        P(("leaf", "panel")),
        P(("leaf", "panel"), None),
        P(("leaf", "panel"), None, None),
        P(("leaf", "panel"), None, None),
        P(("leaf", "panel"), None, None),
    )
    return jax.shard_map(
        local,
        mesh=mesh,
        in_specs=placed,
        out_specs=(P("leaf", "panel", None), P(("leaf", "panel"), None, None)),
        check_vma=False,
    )
```

```python
import jax
import jax.numpy as jnp
from jax import lax
from jax.sharding import PartitionSpec as P


def xor_gather(block, axes, count, groups):
    held = block[None]
    for bits in groups:
        parts = [held]
        for k in range(1, 1 << len(bits)):
            v = sum(((k >> t) & 1) << b for t, b in enumerate(bits))
            parts.append(lax.ppermute(held, axes, [(i, i ^ v) for i in range(count)]))
        held = jnp.concatenate(parts, 0)
    return held


def xor_position(offset, groups):
    position = jnp.zeros_like(offset)
    stride = 1
    for bits in groups:
        k = sum(((offset >> b) & 1) << t for t, b in enumerate(bits))
        position = position + k * stride
        stride *= 1 << len(bits)
    return position


def log2(count):
    bits = count.bit_length() - 1
    assert (1 << bits) == count
    return bits


def local(
    upper_rhs,
    upper_panel,
    upper_inverse,
    top_index,
    top_solution,
    owner_map,
    parent_list,
    lower_index,
    lower_panel,
    lower_rhs,
    lower_inverse,
):
    highest = lax.Precision.HIGHEST
    leaves = lax.axis_size("leaf")
    panels = lax.axis_size("panel")
    count = leaves * panels
    both = ("leaf", "panel")
    me = lax.axis_index(both)
    panel_index = lax.axis_index("panel")
    width_upper = upper_rhs.shape[1]
    share = width_upper // panels
    begin = panel_index * share

    panel_bits = list(range(log2(panels)))
    leaf_bits = list(range(log2(panels), log2(count)))
    high_first = leaf_bits[::-1]
    leaf_groups = []
    if len(high_first) % 2:
        leaf_groups.append([high_first[0]])
        high_first = high_first[1:]
    leaf_groups += [high_first[i : i + 2] for i in range(0, len(high_first), 2)]
    top_groups = [panel_bits] + leaf_groups
    spread_groups = leaf_groups + [[b] for b in panel_bits[::-1]]

    top_rows = top_solution.shape[0]
    top_held = xor_gather(top_solution, both, count, top_groups)
    top_held = top_held.reshape(count * top_rows, top_solution.shape[1])
    wanted = top_index[0]
    source = wanted // top_rows
    slot = xor_position(source ^ me, top_groups) * top_rows + wanted % top_rows
    gathered = top_held[slot]

    folded = jnp.einsum("kv,vw->kw", upper_panel[0], upper_inverse[0], precision=highest)
    own_inverse = lax.dynamic_slice_in_dim(upper_inverse[0], begin, share, 1)
    own_base = jnp.einsum("kw,kr->wr", own_inverse, upper_rhs[0], precision=highest)
    term = jnp.einsum("kw,kr->wr", folded, gathered, precision=highest)
    total = lax.dynamic_slice_in_dim(term, begin, share, 0)
    for v in range(1, panels):
        outgoing = lax.dynamic_slice_in_dim(term, (panel_index ^ v) * share, share, 0)
        total = total + lax.ppermute(outgoing, "panel", [(i, i ^ v) for i in range(panels)])
    own_rows = own_base - total

    lower_base = jnp.einsum("skw,skr->swr", lower_inverse, lower_rhs, precision=highest)
    chained = jnp.einsum("skv,svw->skw", lower_panel, lower_inverse, precision=highest)
    columns = lax.broadcasted_iota(jnp.int32, lower_index.shape + (width_upper,), 2)
    pick = (lower_index[:, :, None] == columns).astype(jnp.float32)
    spread = jnp.einsum("skj,skw->sjw", pick, chained, precision=highest)

    held = xor_gather(own_rows, both, count, spread_groups)
    position = owner_map[parent_list]
    sources = position[:, None] * panels + jnp.arange(panels, dtype=jnp.int32)[None, :]
    slabs = held[xor_position(sources ^ me, spread_groups)]
    slabs = slabs.reshape(position.shape[0], width_upper, own_rows.shape[1])
    lower_update = jnp.einsum("sjw,sjr->swr", spread, slabs, precision=highest)
    lower_solution = lower_base - lower_update
    return (own_rows[None], lower_solution)


def solution(mesh):
    placed = (
        P("leaf", None, None),
        P("leaf", "panel", None),
        P("leaf", None, None),
        P("leaf", "panel"),
        P(("leaf", "panel"), None),
        P(),
        P(("leaf", "panel")),
        P(("leaf", "panel"), None),
        P(("leaf", "panel"), None, None),
        P(("leaf", "panel"), None, None),
        P(("leaf", "panel"), None, None),
    )
    return jax.shard_map(
        local,
        mesh=mesh,
        in_specs=placed,
        out_specs=(P("leaf", "panel", None), P(("leaf", "panel"), None, None)),
        check_vma=False,
    )
```

```python
import jax
import jax.numpy as jnp
from jax import lax
from jax.sharding import PartitionSpec as P


def xor_gather(block, axes, count, groups):
    held = block[None]
    for bits in groups:
        parts = [held]
        for k in range(1, 1 << len(bits)):
            v = sum(((k >> t) & 1) << b for t, b in enumerate(bits))
            parts.append(lax.ppermute(held, axes, [(i, i ^ v) for i in range(count)]))
        held = jnp.concatenate(parts, 0)
    return held


def xor_position(offset, groups):
    position = jnp.zeros_like(offset)
    stride = 1
    for bits in groups:
        k = sum(((offset >> b) & 1) << t for t, b in enumerate(bits))
        position = position + k * stride
        stride *= 1 << len(bits)
    return position


def xor_offset(position, groups):
    offset = jnp.zeros_like(position)
    stride = 1
    for bits in groups:
        k = (position // stride) % (1 << len(bits))
        for t, b in enumerate(bits):
            offset = offset | (((k >> t) & 1) << b)
        stride *= 1 << len(bits)
    return offset


def static_offset(position, groups):
    offset, stride = 0, 1
    for bits in groups:
        k = (position // stride) % (1 << len(bits))
        offset |= sum(((k >> t) & 1) << b for t, b in enumerate(bits))
        stride *= 1 << len(bits)
    return offset


def static_position(offset, groups):
    position, stride = 0, 1
    for bits in groups:
        position += sum(((offset >> b) & 1) << t for t, b in enumerate(bits)) * stride
        stride *= 1 << len(bits)
    return position


def log2(count):
    bits = count.bit_length() - 1
    assert (1 << bits) == count
    return bits


def local(
    upper_rhs,
    upper_panel,
    upper_inverse,
    top_index,
    top_solution,
    owner_map,
    parent_list,
    lower_index,
    lower_panel,
    lower_rhs,
    lower_inverse,
):
    highest = lax.Precision.HIGHEST
    leaves = lax.axis_size("leaf")
    panels = lax.axis_size("panel")
    count = leaves * panels
    both = ("leaf", "panel")
    me = lax.axis_index(both)
    panel_index = lax.axis_index("panel")
    width_upper = upper_rhs.shape[1]
    share = width_upper // panels
    begin = panel_index * share

    panel_bits = list(range(log2(panels)))
    leaf_bits = list(range(log2(panels), log2(count)))
    high_first = leaf_bits[::-1]
    leaf_groups = []
    if len(high_first) % 2:
        leaf_groups.append([high_first[0]])
        high_first = high_first[1:]
    leaf_groups += [high_first[i : i + 2] for i in range(0, len(high_first), 2)]
    top_groups = [panel_bits] + leaf_groups
    spread_groups = leaf_groups + [[b] for b in panel_bits[::-1]]

    top_rows, rhs = top_solution.shape
    places = lax.broadcasted_iota(jnp.int32, (count, top_rows), 0)
    within = lax.broadcasted_iota(jnp.int32, (count, top_rows), 1)
    natural = ((me ^ xor_offset(places, top_groups)) * top_rows + within).reshape(-1)
    pick_top = (top_index[0][:, None] == natural[None, :]).astype(jnp.float32)
    folded = jnp.einsum("kv,vw->kw", upper_panel[0], upper_inverse[0], precision=highest)
    weights = jnp.einsum("kj,kw->wj", pick_top, folded, precision=highest)
    total = lax.dynamic_slice_in_dim(weights, begin, share, 0)
    for v in range(1, panels):
        outgoing = lax.dynamic_slice_in_dim(weights, (panel_index ^ v) * share, share, 0)
        order = [static_position(static_offset(h, top_groups) ^ v, top_groups) for h in range(count)]
        outgoing = outgoing.reshape(share, count, top_rows)[:, jnp.array(order), :]
        outgoing = outgoing.reshape(share, count * top_rows)
        total = total + lax.ppermute(outgoing, "panel", [(i, i ^ v) for i in range(panels)])
    own_inverse = lax.dynamic_slice_in_dim(upper_inverse[0], begin, share, 1)
    own_base = jnp.einsum("kw,kr->wr", own_inverse, upper_rhs[0], precision=highest)

    lower_base = jnp.einsum("skw,skr->swr", lower_inverse, lower_rhs, precision=highest)
    chained = jnp.einsum("skv,svw->skw", lower_panel, lower_inverse, precision=highest)
    columns = lax.broadcasted_iota(jnp.int32, lower_index.shape + (width_upper,), 2)
    pick = (lower_index[:, :, None] == columns).astype(jnp.float32)
    spread = jnp.einsum("skw,skj->swj", chained, pick, precision=highest)

    top_held = xor_gather(top_solution, both, count, top_groups).reshape(count * top_rows, rhs)
    own_rows = own_base - jnp.einsum("wj,jr->wr", total, top_held, precision=highest)

    held = xor_gather(own_rows, both, count, spread_groups)
    position = owner_map[parent_list]
    sources = position[:, None] * panels + jnp.arange(panels, dtype=jnp.int32)[None, :]
    slabs = held[xor_position(sources ^ me, spread_groups)]
    slabs = slabs.reshape(position.shape[0], width_upper, own_rows.shape[1])
    lower_update = jnp.einsum("swj,sjr->swr", spread, slabs, precision=highest)
    lower_solution = lower_base - lower_update
    return (own_rows[None], lower_solution)


def solution(mesh):
    placed = (
        P("leaf", None, None),
        P("leaf", "panel", None),
        P("leaf", None, None),
        P("leaf", "panel"),
        P(("leaf", "panel"), None),
        P(),
        P(("leaf", "panel")),
        P(("leaf", "panel"), None),
        P(("leaf", "panel"), None, None),
        P(("leaf", "panel"), None, None),
        P(("leaf", "panel"), None, None),
    )
    return jax.shard_map(
        local,
        mesh=mesh,
        in_specs=placed,
        out_specs=(P("leaf", "panel", None), P(("leaf", "panel"), None, None)),
        check_vma=False,
    )
```

```python
import jax
import jax.numpy as jnp
from jax import lax
from jax.sharding import PartitionSpec as P


def xor_gather(block, axes, count, groups):
    held = block[None]
    for bits in groups:
        held = xor_gather_step(held, axes, count, bits)
    return held


def xor_gather_step(held, axes, count, bits):
    parts = [held]
    for k in range(1, 1 << len(bits)):
        v = sum(((k >> t) & 1) << b for t, b in enumerate(bits))
        parts.append(lax.ppermute(held, axes, [(i, i ^ v) for i in range(count)]))
    return jnp.concatenate(parts, 0)


def xor_position(offset, groups):
    position = jnp.zeros_like(offset)
    stride = 1
    for bits in groups:
        k = sum(((offset >> b) & 1) << t for t, b in enumerate(bits))
        position = position + k * stride
        stride *= 1 << len(bits)
    return position


def xor_offset(position, groups):
    offset = jnp.zeros_like(position)
    stride = 1
    for bits in groups:
        k = (position // stride) % (1 << len(bits))
        for t, b in enumerate(bits):
            offset = offset | (((k >> t) & 1) << b)
        stride *= 1 << len(bits)
    return offset


def static_offset(position, groups):
    offset, stride = 0, 1
    for bits in groups:
        k = (position // stride) % (1 << len(bits))
        offset |= sum(((k >> t) & 1) << b for t, b in enumerate(bits))
        stride *= 1 << len(bits)
    return offset


def static_position(offset, groups):
    position, stride = 0, 1
    for bits in groups:
        position += sum(((offset >> b) & 1) << t for t, b in enumerate(bits)) * stride
        stride *= 1 << len(bits)
    return position


def log2(count):
    bits = count.bit_length() - 1
    assert (1 << bits) == count
    return bits


def local(
    upper_rhs,
    upper_panel,
    upper_inverse,
    top_index,
    top_solution,
    owner_map,
    parent_list,
    lower_index,
    lower_panel,
    lower_rhs,
    lower_inverse,
):
    highest = lax.Precision.HIGHEST
    leaves = lax.axis_size("leaf")
    panels = lax.axis_size("panel")
    count = leaves * panels
    both = ("leaf", "panel")
    me = lax.axis_index(both)
    panel_index = lax.axis_index("panel")
    width_upper = upper_rhs.shape[1]
    share = width_upper // panels
    begin = panel_index * share

    panel_bits = list(range(log2(panels)))
    leaf_bits = list(range(log2(panels), log2(count)))
    high_first = leaf_bits[::-1]
    leaf_groups = []
    if len(high_first) % 2:
        leaf_groups.append([high_first[0]])
        high_first = high_first[1:]
    leaf_groups += [high_first[i : i + 2] for i in range(0, len(high_first), 2)]
    top_groups = [panel_bits] + leaf_groups
    spread_groups = leaf_groups + [[b] for b in panel_bits[::-1]]

    top_rows, rhs = top_solution.shape
    places = lax.broadcasted_iota(jnp.int32, (count, top_rows), 0)
    within = lax.broadcasted_iota(jnp.int32, (count, top_rows), 1)
    natural = ((me ^ xor_offset(places, top_groups)) * top_rows + within).reshape(-1)
    pick_top = (top_index[0][:, None] == natural[None, :]).astype(jnp.float32)
    folded = jnp.einsum("kv,vw->kw", upper_panel[0], upper_inverse[0], precision=highest)
    weights = jnp.einsum("kj,kw->wj", pick_top, folded, precision=highest)
    total = lax.dynamic_slice_in_dim(weights, begin, share, 0)
    for v in range(1, panels):
        outgoing = lax.dynamic_slice_in_dim(weights, (panel_index ^ v) * share, share, 0)
        order = [static_position(static_offset(h, top_groups) ^ v, top_groups) for h in range(count)]
        outgoing = outgoing.reshape(share, count, top_rows)[:, jnp.array(order), :]
        outgoing = outgoing.reshape(share, count * top_rows)
        total = total + lax.ppermute(outgoing, "panel", [(i, i ^ v) for i in range(panels)])
    own_inverse = lax.dynamic_slice_in_dim(upper_inverse[0], begin, share, 1)
    own_base = jnp.einsum("kw,kr->wr", own_inverse, upper_rhs[0], precision=highest)

    lower_base = jnp.einsum("skw,skr->swr", lower_inverse, lower_rhs, precision=highest)
    chained = jnp.einsum("skv,svw->skw", lower_panel, lower_inverse, precision=highest)
    columns = lax.broadcasted_iota(jnp.int32, lower_index.shape + (width_upper,), 2)
    pick = (lower_index[:, :, None] == columns).astype(jnp.float32)
    spread = jnp.einsum("skw,skj->swj", chained, pick, precision=highest)

    top_held = xor_gather(top_solution, both, count, top_groups).reshape(count * top_rows, rhs)
    top_held, spread, lower_base = lax.optimization_barrier((top_held, spread, lower_base))
    own_rows = own_base - jnp.einsum("wj,jr->wr", total, top_held, precision=highest)

    position = owner_map[parent_list]
    held = xor_gather(own_rows, both, count, leaf_groups)
    present = [0]
    lower_update = None
    for step in [None] + [[b] for b in panel_bits[::-1]]:
        if step is None:
            fresh = present
        else:
            held = xor_gather_step(held, both, count, step)
            fresh = [o ^ (1 << step[0]) for o in present]
            present = present + fresh
        for o in fresh:
            quarter = panel_index ^ o
            blocks = held[xor_position((position * panels + quarter) ^ me, spread_groups)]
            part = lax.dynamic_slice_in_dim(spread, quarter * share, share, 2)
            term = jnp.einsum("swj,sjr->swr", part, blocks, precision=highest)
            lower_update = term if lower_update is None else lower_update + term
    lower_solution = lower_base - lower_update
    return (own_rows[None], lower_solution)


def solution(mesh):
    placed = (
        P("leaf", None, None),
        P("leaf", "panel", None),
        P("leaf", None, None),
        P("leaf", "panel"),
        P(("leaf", "panel"), None),
        P(),
        P(("leaf", "panel")),
        P(("leaf", "panel"), None),
        P(("leaf", "panel"), None, None),
        P(("leaf", "panel"), None, None),
        P(("leaf", "panel"), None, None),
    )
    return jax.shard_map(
        local,
        mesh=mesh,
        in_specs=placed,
        out_specs=(P("leaf", "panel", None), P(("leaf", "panel"), None, None)),
        check_vma=False,
    )
```

```python
import jax
import jax.numpy as jnp
from jax import lax
from jax.sharding import PartitionSpec as P


def xor_gather(block, axes, count, groups):
    held = block[None]
    for bits in groups:
        parts = [held]
        for k in range(1, 1 << len(bits)):
            v = sum(((k >> t) & 1) << b for t, b in enumerate(bits))
            parts.append(lax.ppermute(held, axes, [(i, i ^ v) for i in range(count)]))
        held = jnp.concatenate(parts, 0)
    return held


def xor_position(offset, groups):
    position = jnp.zeros_like(offset)
    stride = 1
    for bits in groups:
        k = sum(((offset >> b) & 1) << t for t, b in enumerate(bits))
        position = position + k * stride
        stride *= 1 << len(bits)
    return position


def xor_offset(position, groups):
    offset = jnp.zeros_like(position)
    stride = 1
    for bits in groups:
        k = (position // stride) % (1 << len(bits))
        for t, b in enumerate(bits):
            offset = offset | (((k >> t) & 1) << b)
        stride *= 1 << len(bits)
    return offset


def static_offset(position, groups):
    offset, stride = 0, 1
    for bits in groups:
        k = (position // stride) % (1 << len(bits))
        offset |= sum(((k >> t) & 1) << b for t, b in enumerate(bits))
        stride *= 1 << len(bits)
    return offset


def static_position(offset, groups):
    position, stride = 0, 1
    for bits in groups:
        position += sum(((offset >> b) & 1) << t for t, b in enumerate(bits)) * stride
        stride *= 1 << len(bits)
    return position


def log2(count):
    bits = count.bit_length() - 1
    assert (1 << bits) == count
    return bits


def local(
    upper_rhs,
    upper_panel,
    upper_inverse,
    top_index,
    top_solution,
    owner_map,
    parent_list,
    lower_index,
    lower_panel,
    lower_rhs,
    lower_inverse,
):
    highest = lax.Precision.HIGHEST
    leaves = lax.axis_size("leaf")
    panels = lax.axis_size("panel")
    count = leaves * panels
    both = ("leaf", "panel")
    me = lax.axis_index(both)
    panel_index = lax.axis_index("panel")
    width_upper = upper_rhs.shape[1]
    share = width_upper // panels
    begin = panel_index * share

    panel_bits = list(range(log2(panels)))
    leaf_bits = list(range(log2(panels), log2(count)))
    high_first = leaf_bits[::-1]
    leaf_groups = []
    if len(high_first) % 2:
        leaf_groups.append([high_first[0]])
        high_first = high_first[1:]
    leaf_groups += [high_first[i : i + 2] for i in range(0, len(high_first), 2)]
    top_groups = [panel_bits] + leaf_groups
    spread_groups = leaf_groups + [[b] for b in panel_bits[::-1]]

    top_rows, rhs = top_solution.shape
    places = lax.broadcasted_iota(jnp.int32, (count, top_rows), 0)
    within = lax.broadcasted_iota(jnp.int32, (count, top_rows), 1)
    natural = ((me ^ xor_offset(places, top_groups)) * top_rows + within).reshape(-1)
    pick_top = (top_index[0][:, None] == natural[None, :]).astype(jnp.float32)
    folded = jnp.einsum("kv,vw->kw", upper_panel[0], upper_inverse[0], precision=highest)
    weights = jnp.einsum("kj,kw->wj", pick_top, folded, precision=highest)
    total = lax.dynamic_slice_in_dim(weights, begin, share, 0)
    for v in range(1, panels):
        outgoing = lax.dynamic_slice_in_dim(weights, (panel_index ^ v) * share, share, 0)
        order = [static_position(static_offset(h, top_groups) ^ v, top_groups) for h in range(count)]
        outgoing = outgoing.reshape(share, count, top_rows)[:, jnp.array(order), :]
        outgoing = outgoing.reshape(share, count * top_rows)
        total = total + lax.ppermute(outgoing, "panel", [(i, i ^ v) for i in range(panels)])
    own_inverse = lax.dynamic_slice_in_dim(upper_inverse[0], begin, share, 1)
    own_base = jnp.einsum("kw,kr->wr", own_inverse, upper_rhs[0], precision=highest)

    top_held = xor_gather(top_solution, both, count, top_groups).reshape(count * top_rows, rhs)
    own_rows = own_base - jnp.einsum("wj,jr->wr", total, top_held, precision=highest)

    held = xor_gather(own_rows, both, count, spread_groups)
    position = owner_map[parent_list]
    sources = position[:, None] * panels + jnp.arange(panels, dtype=jnp.int32)[None, :]
    places = xor_position(sources ^ me, spread_groups)
    slabs = jnp.stack(
        [
            jnp.concatenate([held[places[s, q]] for q in range(panels)], 0)
            for s in range(position.shape[0])
        ]
    )

    columns = lax.broadcasted_iota(jnp.int32, lower_index.shape + (width_upper,), 2)
    pick = (lower_index[:, :, None] == columns).astype(jnp.float32)
    parent_rows = jnp.einsum("skj,sjr->skr", pick, slabs, precision=highest)

    lower_update = jnp.einsum("skw,skr->swr", lower_panel, parent_rows, precision=highest)
    lower_solution = jnp.einsum(
        "skw,skr->swr", lower_inverse, lower_rhs - lower_update, precision=highest
    )
    return (own_rows[None], lower_solution)


def solution(mesh):
    placed = (
        P("leaf", None, None),
        P("leaf", "panel", None),
        P("leaf", None, None),
        P("leaf", "panel"),
        P(("leaf", "panel"), None),
        P(),
        P(("leaf", "panel")),
        P(("leaf", "panel"), None),
        P(("leaf", "panel"), None, None),
        P(("leaf", "panel"), None, None),
        P(("leaf", "panel"), None, None),
    )
    return jax.shard_map(
        local,
        mesh=mesh,
        in_specs=placed,
        out_specs=(P("leaf", "panel", None), P(("leaf", "panel"), None, None)),
        check_vma=False,
    )
```

```python
import jax
import jax.numpy as jnp
from jax import lax
from jax.sharding import PartitionSpec as P


def xor_gather(block, axes, count, groups):
    held = block[None]
    for bits in groups:
        parts = [held]
        for k in range(1, 1 << len(bits)):
            v = sum(((k >> t) & 1) << b for t, b in enumerate(bits))
            parts.append(lax.ppermute(held, axes, [(i, i ^ v) for i in range(count)]))
        held = jnp.concatenate(parts, 0)
    return held


def xor_position(offset, groups):
    position = jnp.zeros_like(offset)
    stride = 1
    for bits in groups:
        k = sum(((offset >> b) & 1) << t for t, b in enumerate(bits))
        position = position + k * stride
        stride *= 1 << len(bits)
    return position


def xor_offset(position, groups):
    offset = jnp.zeros_like(position)
    stride = 1
    for bits in groups:
        k = (position // stride) % (1 << len(bits))
        for t, b in enumerate(bits):
            offset = offset | (((k >> t) & 1) << b)
        stride *= 1 << len(bits)
    return offset


def static_offset(position, groups):
    offset, stride = 0, 1
    for bits in groups:
        k = (position // stride) % (1 << len(bits))
        offset |= sum(((k >> t) & 1) << b for t, b in enumerate(bits))
        stride *= 1 << len(bits)
    return offset


def static_position(offset, groups):
    position, stride = 0, 1
    for bits in groups:
        position += sum(((offset >> b) & 1) << t for t, b in enumerate(bits)) * stride
        stride *= 1 << len(bits)
    return position


def log2(count):
    bits = count.bit_length() - 1
    assert (1 << bits) == count
    return bits


def local(
    upper_rhs,
    upper_panel,
    upper_inverse,
    top_index,
    top_solution,
    owner_map,
    parent_list,
    lower_index,
    lower_panel,
    lower_rhs,
    lower_inverse,
):
    highest = lax.Precision.HIGHEST
    leaves = lax.axis_size("leaf")
    panels = lax.axis_size("panel")
    count = leaves * panels
    both = ("leaf", "panel")
    me = lax.axis_index(both)
    panel_index = lax.axis_index("panel")
    width_upper = upper_rhs.shape[1]
    share = width_upper // panels
    begin = panel_index * share

    panel_bits = list(range(log2(panels)))
    leaf_bits = list(range(log2(panels), log2(count)))
    high_first = leaf_bits[::-1]
    leaf_groups = []
    if len(high_first) % 2:
        leaf_groups.append([high_first[0]])
        high_first = high_first[1:]
    leaf_groups += [high_first[i : i + 2] for i in range(0, len(high_first), 2)]
    top_groups = [panel_bits] + leaf_groups
    spread_groups = leaf_groups + [[b] for b in panel_bits[::-1]]

    top_rows, rhs = top_solution.shape
    places = lax.broadcasted_iota(jnp.int32, (count, top_rows), 0)
    within = lax.broadcasted_iota(jnp.int32, (count, top_rows), 1)
    natural = ((me ^ xor_offset(places, top_groups)) * top_rows + within).reshape(-1)
    pick_top = (top_index[0][:, None] == natural[None, :]).astype(jnp.float32)
    folded = jnp.einsum("kv,vw->kw", upper_panel[0], upper_inverse[0], precision=highest)
    weights = jnp.einsum("kj,kw->wj", pick_top, folded, precision=highest)
    total = lax.dynamic_slice_in_dim(weights, begin, share, 0)
    for v in range(1, panels):
        outgoing = lax.dynamic_slice_in_dim(weights, (panel_index ^ v) * share, share, 0)
        order = [static_position(static_offset(h, top_groups) ^ v, top_groups) for h in range(count)]
        outgoing = outgoing.reshape(share, count, top_rows)[:, jnp.array(order), :]
        outgoing = outgoing.reshape(share, count * top_rows)
        total = total + lax.ppermute(outgoing, "panel", [(i, i ^ v) for i in range(panels)])
    own_inverse = lax.dynamic_slice_in_dim(upper_inverse[0], begin, share, 1)
    own_base = jnp.einsum("kw,kr->wr", own_inverse, upper_rhs[0], precision=highest)

    top_held = xor_gather(top_solution, both, count, top_groups).reshape(count * top_rows, rhs)
    own_rows = own_base - jnp.einsum("wj,jr->wr", total, top_held, precision=highest)

    held = xor_gather(own_rows, both, count, spread_groups)
    position = owner_map[parent_list]
    sources = position[:, None] * panels + jnp.arange(panels, dtype=jnp.int32)[None, :]
    places = xor_position(sources ^ me, spread_groups)
    slabs = held[places].reshape(position.shape[0], width_upper, own_rows.shape[1])

    columns = lax.broadcasted_iota(jnp.int32, lower_index.shape + (width_upper,), 2)
    pick = (lower_index[:, :, None] == columns).astype(jnp.float32)
    parent_rows = jnp.einsum("skj,sjr->skr", pick, slabs, precision=highest)

    lower_update = jnp.einsum("skw,skr->swr", lower_panel, parent_rows, precision=highest)
    lower_solution = jnp.einsum(
        "skw,skr->swr", lower_inverse, lower_rhs - lower_update, precision=highest
    )
    return (own_rows[None], lower_solution)


def solution(mesh):
    placed = (
        P("leaf", None, None),
        P("leaf", "panel", None),
        P("leaf", None, None),
        P("leaf", "panel"),
        P(("leaf", "panel"), None),
        P(),
        P(("leaf", "panel")),
        P(("leaf", "panel"), None),
        P(("leaf", "panel"), None, None),
        P(("leaf", "panel"), None, None),
        P(("leaf", "panel"), None, None),
    )
    return jax.shard_map(
        local,
        mesh=mesh,
        in_specs=placed,
        out_specs=(P("leaf", "panel", None), P(("leaf", "panel"), None, None)),
        check_vma=False,
    )
```

```python
import jax
import jax.numpy as jnp
from jax import lax
from jax.sharding import PartitionSpec as P


def xor_gather(block, axes, count, groups):
    held = block[None]
    for bits in groups:
        parts = [held]
        for k in range(1, 1 << len(bits)):
            v = sum(((k >> t) & 1) << b for t, b in enumerate(bits))
            parts.append(lax.ppermute(held, axes, [(i, i ^ v) for i in range(count)]))
        held = jnp.concatenate(parts, 0)
    return held


def xor_position(offset, groups):
    position = jnp.zeros_like(offset)
    stride = 1
    for bits in groups:
        k = sum(((offset >> b) & 1) << t for t, b in enumerate(bits))
        position = position + k * stride
        stride *= 1 << len(bits)
    return position


def xor_offset(position, groups):
    offset = jnp.zeros_like(position)
    stride = 1
    for bits in groups:
        k = (position // stride) % (1 << len(bits))
        for t, b in enumerate(bits):
            offset = offset | (((k >> t) & 1) << b)
        stride *= 1 << len(bits)
    return offset


def static_offset(position, groups):
    offset, stride = 0, 1
    for bits in groups:
        k = (position // stride) % (1 << len(bits))
        offset |= sum(((k >> t) & 1) << b for t, b in enumerate(bits))
        stride *= 1 << len(bits)
    return offset


def static_position(offset, groups):
    position, stride = 0, 1
    for bits in groups:
        position += sum(((offset >> b) & 1) << t for t, b in enumerate(bits)) * stride
        stride *= 1 << len(bits)
    return position


def log2(count):
    bits = count.bit_length() - 1
    assert (1 << bits) == count
    return bits


def local(
    upper_rhs,
    upper_panel,
    upper_inverse,
    top_index,
    top_solution,
    owner_map,
    parent_list,
    lower_index,
    lower_panel,
    lower_rhs,
    lower_inverse,
):
    highest = lax.Precision.HIGHEST
    leaves = lax.axis_size("leaf")
    panels = lax.axis_size("panel")
    count = leaves * panels
    both = ("leaf", "panel")
    me = lax.axis_index(both)
    panel_index = lax.axis_index("panel")
    width_upper = upper_rhs.shape[1]
    share = width_upper // panels
    begin = panel_index * share

    panel_bits = list(range(log2(panels)))
    leaf_bits = list(range(log2(panels), log2(count)))
    high_first = leaf_bits[::-1]
    leaf_groups = []
    if len(high_first) % 2:
        leaf_groups.append([high_first[0]])
        high_first = high_first[1:]
    leaf_groups += [high_first[i : i + 2] for i in range(0, len(high_first), 2)]
    top_groups = [panel_bits] + leaf_groups
    spread_groups = leaf_groups + [[b] for b in panel_bits[::-1]]

    top_rows, rhs = top_solution.shape
    places = lax.broadcasted_iota(jnp.int32, (count, top_rows), 0)
    within = lax.broadcasted_iota(jnp.int32, (count, top_rows), 1)
    natural = ((me ^ xor_offset(places, top_groups)) * top_rows + within).reshape(-1)
    pick_top = (top_index[0][:, None] == natural[None, :]).astype(jnp.float32)
    folded = jnp.einsum("kv,vw->kw", upper_panel[0], upper_inverse[0], precision=highest)
    weights = jnp.einsum("kj,kw->wj", pick_top, folded, precision=highest)

    def to_partner(block, v):
        order = [static_position(static_offset(h, top_groups) ^ v, top_groups) for h in range(count)]
        shape = block.shape
        block = block.reshape(shape[:-1] + (count, top_rows))[..., jnp.array(order), :]
        return block.reshape(shape)

    core = panel_index & 1
    halves = panels // 2
    split = weights.reshape(halves, 2, share, count * top_rows)
    mine = lax.dynamic_index_in_dim(split, core, 1, keepdims=False)
    other = lax.dynamic_index_in_dim(split, 1 - core, 1, keepdims=False)
    total = mine + lax.ppermute(to_partner(other, 1), "panel", [(i, i ^ 1) for i in range(panels)])
    for b in panel_bits[1:]:
        v = 1 << b
        total = total + lax.ppermute(to_partner(total, v), "panel", [(i, i ^ v) for i in range(panels)])
    total = total.reshape(halves * share, count * top_rows)
    inverse_split = upper_inverse[0].reshape(width_upper, halves, 2, share)
    own_inverse = lax.dynamic_index_in_dim(inverse_split, core, 2, keepdims=False)
    own_inverse = own_inverse.reshape(width_upper, halves * share)
    own_base = jnp.einsum("kw,kr->wr", own_inverse, upper_rhs[0], precision=highest)

    top_held = xor_gather(top_solution, both, count, top_groups).reshape(count * top_rows, rhs)
    own_half = own_base - jnp.einsum("wj,jr->wr", total, top_held, precision=highest)
    own_rows = lax.dynamic_slice_in_dim(own_half, (panel_index >> 1) * share, share, 0)

    half_groups = leaf_groups + [[0]]
    held = xor_gather(own_half, both, count, half_groups)
    held = held.reshape(-1, share, own_half.shape[1])
    position = owner_map[parent_list]
    quarters = jnp.arange(panels, dtype=jnp.int32)[None, :]
    sources = position[:, None] * panels + ((panel_index & ~1) | (quarters & 1))
    places = xor_position(sources ^ me, half_groups) * halves + (quarters >> 1)
    slabs = held[places].reshape(position.shape[0], width_upper, own_half.shape[1])

    columns = lax.broadcasted_iota(jnp.int32, lower_index.shape + (width_upper,), 2)
    pick = (lower_index[:, :, None] == columns).astype(jnp.float32)
    parent_rows = jnp.einsum("skj,sjr->skr", pick, slabs, precision=highest)

    lower_update = jnp.einsum("skw,skr->swr", lower_panel, parent_rows, precision=highest)
    lower_solution = jnp.einsum(
        "skw,skr->swr", lower_inverse, lower_rhs - lower_update, precision=highest
    )
    return (own_rows[None], lower_solution)


def solution(mesh):
    placed = (
        P("leaf", None, None),
        P("leaf", "panel", None),
        P("leaf", None, None),
        P("leaf", "panel"),
        P(("leaf", "panel"), None),
        P(),
        P(("leaf", "panel")),
        P(("leaf", "panel"), None),
        P(("leaf", "panel"), None, None),
        P(("leaf", "panel"), None, None),
        P(("leaf", "panel"), None, None),
    )
    return jax.shard_map(
        local,
        mesh=mesh,
        in_specs=placed,
        out_specs=(P("leaf", "panel", None), P(("leaf", "panel"), None, None)),
        check_vma=False,
    )
```

```python
import jax
import jax.numpy as jnp
from jax import lax
from jax.sharding import PartitionSpec as P


def xor_gather(block, axes, count, groups):
    held = block[None]
    for bits in groups:
        parts = [held]
        for k in range(1, 1 << len(bits)):
            v = sum(((k >> t) & 1) << b for t, b in enumerate(bits))
            parts.append(lax.ppermute(held, axes, [(i, i ^ v) for i in range(count)]))
        held = jnp.concatenate(parts, 0)
    return held


def xor_position(offset, groups):
    position = jnp.zeros_like(offset)
    stride = 1
    for bits in groups:
        k = sum(((offset >> b) & 1) << t for t, b in enumerate(bits))
        position = position + k * stride
        stride *= 1 << len(bits)
    return position


def xor_offset(position, groups):
    offset = jnp.zeros_like(position)
    stride = 1
    for bits in groups:
        k = (position // stride) % (1 << len(bits))
        for t, b in enumerate(bits):
            offset = offset | (((k >> t) & 1) << b)
        stride *= 1 << len(bits)
    return offset


def static_offset(position, groups):
    offset, stride = 0, 1
    for bits in groups:
        k = (position // stride) % (1 << len(bits))
        offset |= sum(((k >> t) & 1) << b for t, b in enumerate(bits))
        stride *= 1 << len(bits)
    return offset


def static_position(offset, groups):
    position, stride = 0, 1
    for bits in groups:
        position += sum(((offset >> b) & 1) << t for t, b in enumerate(bits)) * stride
        stride *= 1 << len(bits)
    return position


def log2(count):
    bits = count.bit_length() - 1
    assert (1 << bits) == count
    return bits


def local(
    upper_rhs,
    upper_panel,
    upper_inverse,
    top_index,
    top_solution,
    owner_map,
    parent_list,
    lower_index,
    lower_panel,
    lower_rhs,
    lower_inverse,
):
    highest = lax.Precision.HIGHEST
    leaves = lax.axis_size("leaf")
    panels = lax.axis_size("panel")
    count = leaves * panels
    both = ("leaf", "panel")
    me = lax.axis_index(both)
    panel_index = lax.axis_index("panel")
    width_upper = upper_rhs.shape[1]
    share = width_upper // panels
    begin = panel_index * share

    panel_bits = list(range(log2(panels)))
    leaf_bits = list(range(log2(panels), log2(count)))
    high_first = leaf_bits[::-1]
    leaf_groups = []
    if len(high_first) % 2:
        leaf_groups.append([high_first[0]])
        high_first = high_first[1:]
    leaf_groups += [high_first[i : i + 2] for i in range(0, len(high_first), 2)]
    top_groups = [panel_bits] + leaf_groups
    spread_groups = leaf_groups + [[b] for b in panel_bits[::-1]]

    top_rows, rhs = top_solution.shape
    places = lax.broadcasted_iota(jnp.int32, (count, top_rows), 0)
    within = lax.broadcasted_iota(jnp.int32, (count, top_rows), 1)
    natural = ((me ^ xor_offset(places, top_groups)) * top_rows + within).reshape(-1)
    pick_top = (top_index[0][:, None] == natural[None, :]).astype(jnp.float32)
    folded = jnp.einsum("kv,vw->kw", upper_panel[0], upper_inverse[0], precision=highest)
    weights = jnp.einsum("kj,kw->wj", pick_top, folded, precision=highest)
    total = lax.dynamic_slice_in_dim(weights, begin, share, 0)
    for v in range(1, panels):
        outgoing = lax.dynamic_slice_in_dim(weights, (panel_index ^ v) * share, share, 0)
        order = [static_position(static_offset(h, top_groups) ^ v, top_groups) for h in range(count)]
        outgoing = outgoing.reshape(share, count, top_rows)[:, jnp.array(order), :]
        outgoing = outgoing.reshape(share, count * top_rows)
        total = total + lax.ppermute(outgoing, "panel", [(i, i ^ v) for i in range(panels)])
    own_inverse = lax.dynamic_slice_in_dim(upper_inverse[0], begin, share, 1)
    own_base = jnp.einsum("kw,kr->wr", own_inverse, upper_rhs[0], precision=highest)

    top_held = xor_gather(top_solution, both, count, top_groups).reshape(count * top_rows, rhs)
    own_rows = own_base - jnp.einsum("wj,jr->wr", total, top_held, precision=highest)

    held = xor_gather(own_rows, both, count, spread_groups)
    position = owner_map[parent_list]
    sources = position[:, None] * panels + jnp.arange(panels, dtype=jnp.int32)[None, :]
    places = xor_position(sources ^ me, spread_groups)
    slabs = held[places].reshape(position.shape[0], width_upper, own_rows.shape[1])

    three = lax.Precision.HIGH
    columns = lax.broadcasted_iota(jnp.int32, lower_index.shape + (width_upper,), 2)
    pick = (lower_index[:, :, None] == columns).astype(jnp.float32)
    parent_rows = jnp.einsum("skj,sjr->skr", pick, slabs, precision=three)

    panel_t = jnp.swapaxes(lower_panel, 1, 2)
    inverse_t = jnp.swapaxes(lower_inverse, 1, 2)
    lower_update = jnp.einsum("swk,skr->swr", panel_t, parent_rows, precision=three)
    lower_solution = jnp.einsum("swk,skr->swr", inverse_t, lower_rhs - lower_update, precision=three)
    return (own_rows[None], lower_solution)


def solution(mesh):
    placed = (
        P("leaf", None, None),
        P("leaf", "panel", None),
        P("leaf", None, None),
        P("leaf", "panel"),
        P(("leaf", "panel"), None),
        P(),
        P(("leaf", "panel")),
        P(("leaf", "panel"), None),
        P(("leaf", "panel"), None, None),
        P(("leaf", "panel"), None, None),
        P(("leaf", "panel"), None, None),
    )
    return jax.shard_map(
        local,
        mesh=mesh,
        in_specs=placed,
        out_specs=(P("leaf", "panel", None), P(("leaf", "panel"), None, None)),
        check_vma=False,
    )
```

```python
import jax
import jax.numpy as jnp
from jax import lax
from jax.sharding import PartitionSpec as P


def xor_gather(block, axes, count, groups):
    held = block[None]
    for bits in groups:
        parts = [held]
        for k in range(1, 1 << len(bits)):
            v = sum(((k >> t) & 1) << b for t, b in enumerate(bits))
            parts.append(lax.ppermute(held, axes, [(i, i ^ v) for i in range(count)]))
        held = jnp.concatenate(parts, 0)
    return held


def xor_position(offset, groups):
    position = jnp.zeros_like(offset)
    stride = 1
    for bits in groups:
        k = sum(((offset >> b) & 1) << t for t, b in enumerate(bits))
        position = position + k * stride
        stride *= 1 << len(bits)
    return position


def xor_offset(position, groups):
    offset = jnp.zeros_like(position)
    stride = 1
    for bits in groups:
        k = (position // stride) % (1 << len(bits))
        for t, b in enumerate(bits):
            offset = offset | (((k >> t) & 1) << b)
        stride *= 1 << len(bits)
    return offset


def static_offset(position, groups):
    offset, stride = 0, 1
    for bits in groups:
        k = (position // stride) % (1 << len(bits))
        offset |= sum(((k >> t) & 1) << b for t, b in enumerate(bits))
        stride *= 1 << len(bits)
    return offset


def static_position(offset, groups):
    position, stride = 0, 1
    for bits in groups:
        position += sum(((offset >> b) & 1) << t for t, b in enumerate(bits)) * stride
        stride *= 1 << len(bits)
    return position


def log2(count):
    bits = count.bit_length() - 1
    assert (1 << bits) == count
    return bits


def local(
    upper_rhs,
    upper_panel,
    upper_inverse,
    top_index,
    top_solution,
    owner_map,
    parent_list,
    lower_index,
    lower_panel,
    lower_rhs,
    lower_inverse,
):
    highest = lax.Precision.HIGHEST
    leaves = lax.axis_size("leaf")
    panels = lax.axis_size("panel")
    count = leaves * panels
    both = ("leaf", "panel")
    me = lax.axis_index(both)
    panel_index = lax.axis_index("panel")
    width_upper = upper_rhs.shape[1]
    share = width_upper // panels
    begin = panel_index * share

    panel_bits = list(range(log2(panels)))
    leaf_bits = list(range(log2(panels), log2(count)))
    high_first = leaf_bits[::-1]
    leaf_groups = []
    if len(high_first) % 2:
        leaf_groups.append([high_first[0]])
        high_first = high_first[1:]
    leaf_groups += [high_first[i : i + 2] for i in range(0, len(high_first), 2)]
    top_groups = [panel_bits] + leaf_groups
    spread_groups = leaf_groups + [[b] for b in panel_bits[::-1]]

    top_rows, rhs = top_solution.shape
    places = lax.broadcasted_iota(jnp.int32, (count, top_rows), 0)
    within = lax.broadcasted_iota(jnp.int32, (count, top_rows), 1)
    natural = ((me ^ xor_offset(places, top_groups)) * top_rows + within).reshape(-1)
    pick_top = (top_index[0][:, None] == natural[None, :]).astype(jnp.float32)
    folded = jnp.einsum("kv,vw->kw", upper_panel[0], upper_inverse[0], precision=highest)
    weights = jnp.einsum("kj,kw->wj", pick_top, folded, precision=highest)
    total = lax.dynamic_slice_in_dim(weights, begin, share, 0)
    for v in range(1, panels):
        outgoing = lax.dynamic_slice_in_dim(weights, (panel_index ^ v) * share, share, 0)
        order = [static_position(static_offset(h, top_groups) ^ v, top_groups) for h in range(count)]
        outgoing = outgoing.reshape(share, count, top_rows)[:, jnp.array(order), :]
        outgoing = outgoing.reshape(share, count * top_rows)
        total = total + lax.ppermute(outgoing, "panel", [(i, i ^ v) for i in range(panels)])
    own_inverse = lax.dynamic_slice_in_dim(upper_inverse[0], begin, share, 1)
    own_base = jnp.einsum("kw,kr->wr", own_inverse, upper_rhs[0], precision=highest)

    top_held = xor_gather(top_solution, both, count, top_groups).reshape(count * top_rows, rhs)
    own_rows = own_base - jnp.einsum("wj,jr->wr", total, top_held, precision=highest)

    held = xor_gather(own_rows, both, count, spread_groups[:-1])
    last = spread_groups[-1][0]
    partner = lax.ppermute(held, both, [(i, i ^ (1 << last)) for i in range(count)])
    position = owner_map[parent_list]
    parent_rows = None
    for side, source in ((0, held), (1, partner)):
        offsets = jnp.array([o for o in range(panels) if ((o >> last) & 1) == side], jnp.int32)
        quarters = panel_index ^ offsets
        sources = position[:, None] * panels + quarters[None, :]
        places = xor_position(sources ^ me, spread_groups) - side * held.shape[0]
        slabs = source[places].reshape(position.shape[0], -1, own_rows.shape[1])
        within = lax.broadcasted_iota(jnp.int32, (offsets.shape[0], share), 1)
        columns = (quarters[:, None] * share + within).reshape(-1)
        pick = (lower_index[:, :, None] == columns[None, None, :]).astype(jnp.float32)
        term = jnp.einsum("skj,sjr->skr", pick, slabs, precision=highest)
        parent_rows = term if parent_rows is None else parent_rows + term

    panel_t = jnp.swapaxes(lower_panel, 1, 2)
    inverse_t = jnp.swapaxes(lower_inverse, 1, 2)
    lower_update = jnp.einsum("swk,skr->swr", panel_t, parent_rows, precision=highest)
    lower_solution = jnp.einsum(
        "swk,skr->swr", inverse_t, lower_rhs - lower_update, precision=highest
    )
    return (own_rows[None], lower_solution)


def solution(mesh):
    placed = (
        P("leaf", None, None),
        P("leaf", "panel", None),
        P("leaf", None, None),
        P("leaf", "panel"),
        P(("leaf", "panel"), None),
        P(),
        P(("leaf", "panel")),
        P(("leaf", "panel"), None),
        P(("leaf", "panel"), None, None),
        P(("leaf", "panel"), None, None),
        P(("leaf", "panel"), None, None),
    )
    return jax.shard_map(
        local,
        mesh=mesh,
        in_specs=placed,
        out_specs=(P("leaf", "panel", None), P(("leaf", "panel"), None, None)),
        check_vma=False,
    )
```

```python
import jax
import jax.numpy as jnp
from jax import lax
from jax.sharding import PartitionSpec as P


def xor_gather(block, axes, count, groups):
    held = block[None]
    for bits in groups:
        parts = [held]
        for k in range(1, 1 << len(bits)):
            v = sum(((k >> t) & 1) << b for t, b in enumerate(bits))
            parts.append(lax.ppermute(held, axes, [(i, i ^ v) for i in range(count)]))
        held = jnp.concatenate(parts, 0)
    return held


def xor_position(offset, groups):
    position = jnp.zeros_like(offset)
    stride = 1
    for bits in groups:
        k = sum(((offset >> b) & 1) << t for t, b in enumerate(bits))
        position = position + k * stride
        stride *= 1 << len(bits)
    return position


def xor_offset(position, groups):
    offset = jnp.zeros_like(position)
    stride = 1
    for bits in groups:
        k = (position // stride) % (1 << len(bits))
        for t, b in enumerate(bits):
            offset = offset | (((k >> t) & 1) << b)
        stride *= 1 << len(bits)
    return offset


def static_offset(position, groups):
    offset, stride = 0, 1
    for bits in groups:
        k = (position // stride) % (1 << len(bits))
        offset |= sum(((k >> t) & 1) << b for t, b in enumerate(bits))
        stride *= 1 << len(bits)
    return offset


def static_position(offset, groups):
    position, stride = 0, 1
    for bits in groups:
        position += sum(((offset >> b) & 1) << t for t, b in enumerate(bits)) * stride
        stride *= 1 << len(bits)
    return position


def log2(count):
    bits = count.bit_length() - 1
    assert (1 << bits) == count
    return bits


def local(
    upper_rhs,
    upper_panel,
    upper_inverse,
    top_index,
    top_solution,
    owner_map,
    parent_list,
    lower_index,
    lower_panel,
    lower_rhs,
    lower_inverse,
):
    highest = lax.Precision.HIGHEST
    leaves = lax.axis_size("leaf")
    panels = lax.axis_size("panel")
    count = leaves * panels
    both = ("leaf", "panel")
    me = lax.axis_index(both)
    panel_index = lax.axis_index("panel")
    width_upper = upper_rhs.shape[1]
    share = width_upper // panels
    begin = panel_index * share

    panel_bits = list(range(log2(panels)))
    leaf_bits = list(range(log2(panels), log2(count)))
    high_first = leaf_bits[::-1]
    leaf_groups = []
    if len(high_first) % 2:
        leaf_groups.append([high_first[0]])
        high_first = high_first[1:]
    leaf_groups += [high_first[i : i + 2] for i in range(0, len(high_first), 2)]
    top_groups = [panel_bits] + leaf_groups
    spread_groups = [[b] for b in panel_bits[1:]] + leaf_groups + [[0]]

    top_rows, rhs = top_solution.shape
    places = lax.broadcasted_iota(jnp.int32, (count, top_rows), 0)
    within = lax.broadcasted_iota(jnp.int32, (count, top_rows), 1)
    natural = ((me ^ xor_offset(places, top_groups)) * top_rows + within).reshape(-1)
    pick_top = (top_index[0][:, None] == natural[None, :]).astype(jnp.float32)
    folded = jnp.einsum("kv,vw->kw", upper_panel[0], upper_inverse[0], precision=highest)
    weights = jnp.einsum("kj,kw->wj", pick_top, folded, precision=highest)
    total = lax.dynamic_slice_in_dim(weights, begin, share, 0)
    for v in range(1, panels):
        outgoing = lax.dynamic_slice_in_dim(weights, (panel_index ^ v) * share, share, 0)
        order = [static_position(static_offset(h, top_groups) ^ v, top_groups) for h in range(count)]
        outgoing = outgoing.reshape(share, count, top_rows)[:, jnp.array(order), :]
        outgoing = outgoing.reshape(share, count * top_rows)
        total = total + lax.ppermute(outgoing, "panel", [(i, i ^ v) for i in range(panels)])
    own_inverse = lax.dynamic_slice_in_dim(upper_inverse[0], begin, share, 1)
    own_base = jnp.einsum("kw,kr->wr", own_inverse, upper_rhs[0], precision=highest)

    top_held = xor_gather(top_solution, both, count, top_groups).reshape(count * top_rows, rhs)
    own_rows = own_base - jnp.einsum("wj,jr->wr", total, top_held, precision=highest)

    held = xor_gather(own_rows, both, count, spread_groups[:-1])
    last = spread_groups[-1][0]
    partner = lax.ppermute(held, both, [(i, i ^ (1 << last)) for i in range(count)])
    position = owner_map[parent_list]
    parent_rows = None
    for side, source in ((0, held), (1, partner)):
        offsets = jnp.array([o for o in range(panels) if ((o >> last) & 1) == side], jnp.int32)
        quarters = panel_index ^ offsets
        sources = position[:, None] * panels + quarters[None, :]
        places = xor_position(sources ^ me, spread_groups) - side * held.shape[0]
        slabs = source[places].reshape(position.shape[0], -1, own_rows.shape[1])
        within = lax.broadcasted_iota(jnp.int32, (offsets.shape[0], share), 1)
        columns = (quarters[:, None] * share + within).reshape(-1)
        pick = (lower_index[:, :, None] == columns[None, None, :]).astype(jnp.float32)
        term = jnp.einsum("skj,sjr->skr", pick, slabs, precision=highest)
        parent_rows = term if parent_rows is None else parent_rows + term

    panel_t = jnp.swapaxes(lower_panel, 1, 2)
    inverse_t = jnp.swapaxes(lower_inverse, 1, 2)
    lower_update = jnp.einsum("swk,skr->swr", panel_t, parent_rows, precision=highest)
    lower_solution = jnp.einsum(
        "swk,skr->swr", inverse_t, lower_rhs - lower_update, precision=highest
    )
    return (own_rows[None], lower_solution)


def solution(mesh):
    placed = (
        P("leaf", None, None),
        P("leaf", "panel", None),
        P("leaf", None, None),
        P("leaf", "panel"),
        P(("leaf", "panel"), None),
        P(),
        P(("leaf", "panel")),
        P(("leaf", "panel"), None),
        P(("leaf", "panel"), None, None),
        P(("leaf", "panel"), None, None),
        P(("leaf", "panel"), None, None),
    )
    return jax.shard_map(
        local,
        mesh=mesh,
        in_specs=placed,
        out_specs=(P("leaf", "panel", None), P(("leaf", "panel"), None, None)),
        check_vma=False,
    )
```

```python
import jax
import jax.numpy as jnp
from jax import lax
from jax.sharding import PartitionSpec as P


def xor_gather(block, axes, count, groups):
    held = block[None]
    for bits in groups:
        parts = [held]
        for k in range(1, 1 << len(bits)):
            v = sum(((k >> t) & 1) << b for t, b in enumerate(bits))
            parts.append(lax.ppermute(held, axes, [(i, i ^ v) for i in range(count)]))
        held = jnp.concatenate(parts, 0)
    return held


def xor_position(offset, groups):
    position = jnp.zeros_like(offset)
    stride = 1
    for bits in groups:
        k = sum(((offset >> b) & 1) << t for t, b in enumerate(bits))
        position = position + k * stride
        stride *= 1 << len(bits)
    return position


def xor_offset(position, groups):
    offset = jnp.zeros_like(position)
    stride = 1
    for bits in groups:
        k = (position // stride) % (1 << len(bits))
        for t, b in enumerate(bits):
            offset = offset | (((k >> t) & 1) << b)
        stride *= 1 << len(bits)
    return offset


def static_offset(position, groups):
    offset, stride = 0, 1
    for bits in groups:
        k = (position // stride) % (1 << len(bits))
        offset |= sum(((k >> t) & 1) << b for t, b in enumerate(bits))
        stride *= 1 << len(bits)
    return offset


def static_position(offset, groups):
    position, stride = 0, 1
    for bits in groups:
        position += sum(((offset >> b) & 1) << t for t, b in enumerate(bits)) * stride
        stride *= 1 << len(bits)
    return position


def log2(count):
    bits = count.bit_length() - 1
    assert (1 << bits) == count
    return bits


def local(
    upper_rhs,
    upper_panel,
    upper_inverse,
    top_index,
    top_solution,
    owner_map,
    parent_list,
    lower_index,
    lower_panel,
    lower_rhs,
    lower_inverse,
):
    highest = lax.Precision.HIGHEST
    leaves = lax.axis_size("leaf")
    panels = lax.axis_size("panel")
    count = leaves * panels
    both = ("leaf", "panel")
    me = lax.axis_index(both)
    panel_index = lax.axis_index("panel")
    width_upper = upper_rhs.shape[1]
    share = width_upper // panels
    begin = panel_index * share

    panel_bits = list(range(log2(panels)))
    leaf_bits = list(range(log2(panels), log2(count)))
    high_first = leaf_bits[::-1]
    leaf_groups = []
    if len(high_first) % 2:
        leaf_groups.append([high_first[0]])
        high_first = high_first[1:]
    leaf_groups += [high_first[i : i + 2] for i in range(0, len(high_first), 2)]
    top_groups = [panel_bits] + leaf_groups
    spread_groups = [[b] for b in panel_bits[1:]] + leaf_groups + [[0]]

    top_rows, rhs = top_solution.shape
    places = lax.broadcasted_iota(jnp.int32, (count, top_rows), 0)
    within = lax.broadcasted_iota(jnp.int32, (count, top_rows), 1)
    natural = ((me ^ xor_offset(places, top_groups)) * top_rows + within).reshape(-1)
    pick_top = (top_index[0][:, None] == natural[None, :]).astype(jnp.float32)
    folded = jnp.einsum("kv,vw->kw", upper_panel[0], upper_inverse[0], precision=highest)
    weights = jnp.einsum("kj,kw->wj", pick_top, folded, precision=highest)
    total = lax.dynamic_slice_in_dim(weights, begin, share, 0)
    for v in range(1, panels):
        outgoing = lax.dynamic_slice_in_dim(weights, (panel_index ^ v) * share, share, 0)
        order = [static_position(static_offset(h, top_groups) ^ v, top_groups) for h in range(count)]
        outgoing = outgoing.reshape(share, count, top_rows)[:, jnp.array(order), :]
        outgoing = outgoing.reshape(share, count * top_rows)
        total = total + lax.ppermute(outgoing, "panel", [(i, i ^ v) for i in range(panels)])
    own_inverse = lax.dynamic_slice_in_dim(upper_inverse[0], begin, share, 1)
    own_base = jnp.einsum("kw,kr->wr", own_inverse, upper_rhs[0], precision=highest)

    total = lax.optimization_barrier(total)
    top_held = xor_gather(top_solution, both, count, top_groups).reshape(count * top_rows, rhs)
    own_rows = own_base - jnp.einsum("wj,jr->wr", total, top_held, precision=highest)

    held = xor_gather(own_rows, both, count, spread_groups[:-1])
    last = spread_groups[-1][0]
    partner = lax.ppermute(held, both, [(i, i ^ (1 << last)) for i in range(count)])
    position = owner_map[parent_list]
    parent_rows = None
    for side, source in ((0, held), (1, partner)):
        offsets = jnp.array([o for o in range(panels) if ((o >> last) & 1) == side], jnp.int32)
        quarters = panel_index ^ offsets
        sources = position[:, None] * panels + quarters[None, :]
        places = xor_position(sources ^ me, spread_groups) - side * held.shape[0]
        slabs = source[places].reshape(position.shape[0], -1, own_rows.shape[1])
        within = lax.broadcasted_iota(jnp.int32, (offsets.shape[0], share), 1)
        columns = (quarters[:, None] * share + within).reshape(-1)
        pick = (lower_index[:, :, None] == columns[None, None, :]).astype(jnp.float32)
        term = jnp.einsum("skj,sjr->skr", pick, slabs, precision=highest)
        parent_rows = term if parent_rows is None else parent_rows + term

    panel_t = jnp.swapaxes(lower_panel, 1, 2)
    inverse_t = jnp.swapaxes(lower_inverse, 1, 2)
    lower_update = jnp.einsum("swk,skr->swr", panel_t, parent_rows, precision=highest)
    lower_solution = jnp.einsum(
        "swk,skr->swr", inverse_t, lower_rhs - lower_update, precision=highest
    )
    return (own_rows[None], lower_solution)


def solution(mesh):
    placed = (
        P("leaf", None, None),
        P("leaf", "panel", None),
        P("leaf", None, None),
        P("leaf", "panel"),
        P(("leaf", "panel"), None),
        P(),
        P(("leaf", "panel")),
        P(("leaf", "panel"), None),
        P(("leaf", "panel"), None, None),
        P(("leaf", "panel"), None, None),
        P(("leaf", "panel"), None, None),
    )
    return jax.shard_map(
        local,
        mesh=mesh,
        in_specs=placed,
        out_specs=(P("leaf", "panel", None), P(("leaf", "panel"), None, None)),
        check_vma=False,
    )
```

```python
import jax
import jax.numpy as jnp
from jax import lax
from jax.sharding import PartitionSpec as P


def xor_gather(block, axes, count, groups):
    held = block[None]
    for bits in groups:
        held = xor_gather_step(held, axes, count, bits)
    return held


def xor_gather_step(held, axes, count, bits):
    parts = [held]
    for k in range(1, 1 << len(bits)):
        v = sum(((k >> t) & 1) << b for t, b in enumerate(bits))
        parts.append(lax.ppermute(held, axes, [(i, i ^ v) for i in range(count)]))
    return jnp.concatenate(parts, 0)


def xor_position(offset, groups):
    position = jnp.zeros_like(offset)
    stride = 1
    for bits in groups:
        k = sum(((offset >> b) & 1) << t for t, b in enumerate(bits))
        position = position + k * stride
        stride *= 1 << len(bits)
    return position


def xor_offset(position, groups):
    offset = jnp.zeros_like(position)
    stride = 1
    for bits in groups:
        k = (position // stride) % (1 << len(bits))
        for t, b in enumerate(bits):
            offset = offset | (((k >> t) & 1) << b)
        stride *= 1 << len(bits)
    return offset


def static_offset(position, groups):
    offset, stride = 0, 1
    for bits in groups:
        k = (position // stride) % (1 << len(bits))
        offset |= sum(((k >> t) & 1) << b for t, b in enumerate(bits))
        stride *= 1 << len(bits)
    return offset


def static_position(offset, groups):
    position, stride = 0, 1
    for bits in groups:
        position += sum(((offset >> b) & 1) << t for t, b in enumerate(bits)) * stride
        stride *= 1 << len(bits)
    return position


def log2(count):
    bits = count.bit_length() - 1
    assert (1 << bits) == count
    return bits


def local(
    upper_rhs,
    upper_panel,
    upper_inverse,
    top_index,
    top_solution,
    owner_map,
    parent_list,
    lower_index,
    lower_panel,
    lower_rhs,
    lower_inverse,
):
    highest = lax.Precision.HIGHEST
    leaves = lax.axis_size("leaf")
    panels = lax.axis_size("panel")
    count = leaves * panels
    both = ("leaf", "panel")
    me = lax.axis_index(both)
    panel_index = lax.axis_index("panel")
    width_upper = upper_rhs.shape[1]
    share = width_upper // panels
    begin = panel_index * share

    panel_bits = list(range(log2(panels)))
    leaf_bits = list(range(log2(panels), log2(count)))
    high_first = leaf_bits[::-1]
    leaf_groups = []
    if len(high_first) % 2:
        leaf_groups.append([high_first[0]])
        high_first = high_first[1:]
    leaf_groups += [high_first[i : i + 2] for i in range(0, len(high_first), 2)]
    top_groups = [panel_bits] + leaf_groups
    spread_groups = [[b] for b in panel_bits[1:]] + leaf_groups + [[0]]

    top_rows, rhs = top_solution.shape
    places = lax.broadcasted_iota(jnp.int32, (count, top_rows), 0)
    within = lax.broadcasted_iota(jnp.int32, (count, top_rows), 1)
    natural = ((me ^ xor_offset(places, top_groups)) * top_rows + within).reshape(-1)
    pick_top = (top_index[0][:, None] == natural[None, :]).astype(jnp.float32)
    top_first = xor_gather_step(top_solution[None], both, count, top_groups[0])
    top_first, panel_rows = lax.optimization_barrier((top_first, upper_panel[0]))
    folded = jnp.einsum("kv,vw->kw", panel_rows, upper_inverse[0], precision=highest)
    weights = jnp.einsum("kj,kw->wj", pick_top, folded, precision=highest)
    total = lax.dynamic_slice_in_dim(weights, begin, share, 0)
    for v in range(1, panels):
        outgoing = lax.dynamic_slice_in_dim(weights, (panel_index ^ v) * share, share, 0)
        order = [static_position(static_offset(h, top_groups) ^ v, top_groups) for h in range(count)]
        outgoing = outgoing.reshape(share, count, top_rows)[:, jnp.array(order), :]
        outgoing = outgoing.reshape(share, count * top_rows)
        total = total + lax.ppermute(outgoing, "panel", [(i, i ^ v) for i in range(panels)])
    own_inverse = lax.dynamic_slice_in_dim(upper_inverse[0], begin, share, 1)
    own_base = jnp.einsum("kw,kr->wr", own_inverse, upper_rhs[0], precision=highest)

    top_held = top_first
    for bits in top_groups[1:]:
        top_held = xor_gather_step(top_held, both, count, bits)
    top_held = top_held.reshape(count * top_rows, rhs)
    own_rows = own_base - jnp.einsum("wj,jr->wr", total, top_held, precision=highest)

    held = xor_gather(own_rows, both, count, spread_groups[:-1])
    last = spread_groups[-1][0]
    partner = lax.ppermute(held, both, [(i, i ^ (1 << last)) for i in range(count)])
    position = owner_map[parent_list]
    parent_rows = None
    for side, source in ((0, held), (1, partner)):
        offsets = jnp.array([o for o in range(panels) if ((o >> last) & 1) == side], jnp.int32)
        quarters = panel_index ^ offsets
        sources = position[:, None] * panels + quarters[None, :]
        places = xor_position(sources ^ me, spread_groups) - side * held.shape[0]
        slabs = source[places].reshape(position.shape[0], -1, own_rows.shape[1])
        within = lax.broadcasted_iota(jnp.int32, (offsets.shape[0], share), 1)
        columns = (quarters[:, None] * share + within).reshape(-1)
        pick = (lower_index[:, :, None] == columns[None, None, :]).astype(jnp.float32)
        term = jnp.einsum("skj,sjr->skr", pick, slabs, precision=highest)
        parent_rows = term if parent_rows is None else parent_rows + term

    panel_t = jnp.swapaxes(lower_panel, 1, 2)
    inverse_t = jnp.swapaxes(lower_inverse, 1, 2)
    lower_update = jnp.einsum("swk,skr->swr", panel_t, parent_rows, precision=highest)
    lower_solution = jnp.einsum(
        "swk,skr->swr", inverse_t, lower_rhs - lower_update, precision=highest
    )
    return (own_rows[None], lower_solution)


def solution(mesh):
    placed = (
        P("leaf", None, None),
        P("leaf", "panel", None),
        P("leaf", None, None),
        P("leaf", "panel"),
        P(("leaf", "panel"), None),
        P(),
        P(("leaf", "panel")),
        P(("leaf", "panel"), None),
        P(("leaf", "panel"), None, None),
        P(("leaf", "panel"), None, None),
        P(("leaf", "panel"), None, None),
    )
    return jax.shard_map(
        local,
        mesh=mesh,
        in_specs=placed,
        out_specs=(P("leaf", "panel", None), P(("leaf", "panel"), None, None)),
        check_vma=False,
    )
```

```python
import jax
import jax.numpy as jnp
from jax import lax
from jax.sharding import PartitionSpec as P


def xor_gather(block, axes, count, groups):
    held = block[None]
    for bits in groups:
        parts = [held]
        for k in range(1, 1 << len(bits)):
            v = sum(((k >> t) & 1) << b for t, b in enumerate(bits))
            parts.append(lax.ppermute(held, axes, [(i, i ^ v) for i in range(count)]))
        held = jnp.concatenate(parts, 0)
    return held


def xor_position(offset, groups):
    position = jnp.zeros_like(offset)
    stride = 1
    for bits in groups:
        k = sum(((offset >> b) & 1) << t for t, b in enumerate(bits))
        position = position + k * stride
        stride *= 1 << len(bits)
    return position


def xor_offset(position, groups):
    offset = jnp.zeros_like(position)
    stride = 1
    for bits in groups:
        k = (position // stride) % (1 << len(bits))
        for t, b in enumerate(bits):
            offset = offset | (((k >> t) & 1) << b)
        stride *= 1 << len(bits)
    return offset


def static_offset(position, groups):
    offset, stride = 0, 1
    for bits in groups:
        k = (position // stride) % (1 << len(bits))
        offset |= sum(((k >> t) & 1) << b for t, b in enumerate(bits))
        stride *= 1 << len(bits)
    return offset


def static_position(offset, groups):
    position, stride = 0, 1
    for bits in groups:
        position += sum(((offset >> b) & 1) << t for t, b in enumerate(bits)) * stride
        stride *= 1 << len(bits)
    return position


def log2(count):
    bits = count.bit_length() - 1
    assert (1 << bits) == count
    return bits


def local(
    upper_rhs,
    upper_panel,
    upper_inverse,
    top_index,
    top_solution,
    owner_map,
    parent_list,
    lower_index,
    lower_panel,
    lower_rhs,
    lower_inverse,
):
    highest = lax.Precision.HIGHEST
    leaves = lax.axis_size("leaf")
    panels = lax.axis_size("panel")
    count = leaves * panels
    both = ("leaf", "panel")
    me = lax.axis_index(both)
    panel_index = lax.axis_index("panel")
    width_upper = upper_rhs.shape[1]
    share = width_upper // panels
    begin = panel_index * share

    panel_bits = list(range(log2(panels)))
    leaf_bits = list(range(log2(panels), log2(count)))
    high_first = leaf_bits[::-1]
    leaf_groups = []
    if len(high_first) % 2:
        leaf_groups.append([high_first[0]])
        high_first = high_first[1:]
    leaf_groups += [high_first[i : i + 2] for i in range(0, len(high_first), 2)]
    top_groups = [panel_bits] + leaf_groups
    spread_groups = [[b] for b in panel_bits[1:]] + leaf_groups + [[0]]

    top_rows, rhs = top_solution.shape
    places = lax.broadcasted_iota(jnp.int32, (count, top_rows), 0)
    within = lax.broadcasted_iota(jnp.int32, (count, top_rows), 1)
    natural = ((me ^ xor_offset(places, top_groups)) * top_rows + within).reshape(-1)
    pick_top = (top_index[0][:, None] == natural[None, :]).astype(jnp.float32)
    folded = jnp.einsum("kv,vw->kw", upper_panel[0], upper_inverse[0], precision=highest)
    weights = jnp.einsum("kj,kw->wj", pick_top, folded, precision=highest)
    top_block, weights = lax.optimization_barrier((top_solution, weights))
    total = lax.dynamic_slice_in_dim(weights, begin, share, 0)
    for v in range(1, panels):
        outgoing = lax.dynamic_slice_in_dim(weights, (panel_index ^ v) * share, share, 0)
        order = [static_position(static_offset(h, top_groups) ^ v, top_groups) for h in range(count)]
        outgoing = outgoing.reshape(share, count, top_rows)[:, jnp.array(order), :]
        outgoing = outgoing.reshape(share, count * top_rows)
        total = total + lax.ppermute(outgoing, "panel", [(i, i ^ v) for i in range(panels)])
    own_inverse = lax.dynamic_slice_in_dim(upper_inverse[0], begin, share, 1)
    own_base = jnp.einsum("kw,kr->wr", own_inverse, upper_rhs[0], precision=highest)

    top_held = xor_gather(top_block, both, count, top_groups).reshape(count * top_rows, rhs)
    own_rows = own_base - jnp.einsum("wj,jr->wr", total, top_held, precision=highest)

    held = xor_gather(own_rows, both, count, spread_groups[:-1])
    last = spread_groups[-1][0]
    partner = lax.ppermute(held, both, [(i, i ^ (1 << last)) for i in range(count)])
    position = owner_map[parent_list]
    parent_rows = None
    for side, source in ((0, held), (1, partner)):
        offsets = jnp.array([o for o in range(panels) if ((o >> last) & 1) == side], jnp.int32)
        quarters = panel_index ^ offsets
        sources = position[:, None] * panels + quarters[None, :]
        places = xor_position(sources ^ me, spread_groups) - side * held.shape[0]
        slabs = source[places].reshape(position.shape[0], -1, own_rows.shape[1])
        within = lax.broadcasted_iota(jnp.int32, (offsets.shape[0], share), 1)
        columns = (quarters[:, None] * share + within).reshape(-1)
        pick = (lower_index[:, :, None] == columns[None, None, :]).astype(jnp.float32)
        term = jnp.einsum("skj,sjr->skr", pick, slabs, precision=highest)
        parent_rows = term if parent_rows is None else parent_rows + term

    panel_t = jnp.swapaxes(lower_panel, 1, 2)
    inverse_t = jnp.swapaxes(lower_inverse, 1, 2)
    lower_update = jnp.einsum("swk,skr->swr", panel_t, parent_rows, precision=highest)
    lower_solution = jnp.einsum(
        "swk,skr->swr", inverse_t, lower_rhs - lower_update, precision=highest
    )
    return (own_rows[None], lower_solution)


def solution(mesh):
    placed = (
        P("leaf", None, None),
        P("leaf", "panel", None),
        P("leaf", None, None),
        P("leaf", "panel"),
        P(("leaf", "panel"), None),
        P(),
        P(("leaf", "panel")),
        P(("leaf", "panel"), None),
        P(("leaf", "panel"), None, None),
        P(("leaf", "panel"), None, None),
        P(("leaf", "panel"), None, None),
    )
    return jax.shard_map(
        local,
        mesh=mesh,
        in_specs=placed,
        out_specs=(P("leaf", "panel", None), P(("leaf", "panel"), None, None)),
        check_vma=False,
    )
```

```python
import jax
import jax.numpy as jnp
from jax import lax
from jax.sharding import PartitionSpec as P


def xor_gather(block, axes, count, groups):
    held = block[None]
    for bits in groups:
        parts = [held]
        for k in range(1, 1 << len(bits)):
            v = sum(((k >> t) & 1) << b for t, b in enumerate(bits))
            parts.append(lax.ppermute(held, axes, [(i, i ^ v) for i in range(count)]))
        held = jnp.concatenate(parts, 0)
    return held


def xor_position(offset, groups):
    position = jnp.zeros_like(offset)
    stride = 1
    for bits in groups:
        k = sum(((offset >> b) & 1) << t for t, b in enumerate(bits))
        position = position + k * stride
        stride *= 1 << len(bits)
    return position


def xor_offset(position, groups):
    offset = jnp.zeros_like(position)
    stride = 1
    for bits in groups:
        k = (position // stride) % (1 << len(bits))
        for t, b in enumerate(bits):
            offset = offset | (((k >> t) & 1) << b)
        stride *= 1 << len(bits)
    return offset


def static_offset(position, groups):
    offset, stride = 0, 1
    for bits in groups:
        k = (position // stride) % (1 << len(bits))
        offset |= sum(((k >> t) & 1) << b for t, b in enumerate(bits))
        stride *= 1 << len(bits)
    return offset


def static_position(offset, groups):
    position, stride = 0, 1
    for bits in groups:
        position += sum(((offset >> b) & 1) << t for t, b in enumerate(bits)) * stride
        stride *= 1 << len(bits)
    return position


def log2(count):
    bits = count.bit_length() - 1
    assert (1 << bits) == count
    return bits


def local(
    upper_rhs,
    upper_panel,
    upper_inverse,
    top_index,
    top_solution,
    owner_map,
    parent_list,
    lower_index,
    lower_panel,
    lower_rhs,
    lower_inverse,
):
    highest = lax.Precision.HIGHEST
    leaves = lax.axis_size("leaf")
    panels = lax.axis_size("panel")
    count = leaves * panels
    both = ("leaf", "panel")
    me = lax.axis_index(both)
    panel_index = lax.axis_index("panel")
    width_upper = upper_rhs.shape[1]
    share = width_upper // panels
    begin = panel_index * share

    panel_bits = list(range(log2(panels)))
    leaf_bits = list(range(log2(panels), log2(count)))
    high_first = leaf_bits[::-1]
    leaf_groups = []
    if len(high_first) % 2:
        leaf_groups.append([high_first[0]])
        high_first = high_first[1:]
    leaf_groups += [high_first[i : i + 2] for i in range(0, len(high_first), 2)]
    top_groups = [panel_bits] + leaf_groups
    spread_groups = [[b] for b in panel_bits[1:]] + leaf_groups + [[0]]

    top_rows, rhs = top_solution.shape
    places = lax.broadcasted_iota(jnp.int32, (count, top_rows), 0)
    within = lax.broadcasted_iota(jnp.int32, (count, top_rows), 1)
    natural = ((me ^ xor_offset(places, top_groups)) * top_rows + within).reshape(-1)
    pick_top = (top_index[0][:, None] == natural[None, :]).astype(jnp.float32)
    folded = jnp.einsum("kv,vw->kw", upper_panel[0], upper_inverse[0], precision=highest)
    weights = jnp.einsum("kj,kw->wj", pick_top, folded, precision=highest)
    keep = list(range(panels))
    rows = jnp.stack([lax.dynamic_slice_in_dim(weights, (panel_index ^ o) * share, share, 0) for o in keep])
    for b in panel_bits:
        v = 1 << b
        send = [i for i, o in enumerate(keep) if (o >> b) & 1]
        stay = [i for i, o in enumerate(keep) if not (o >> b) & 1]
        order = [static_position(static_offset(h, top_groups) ^ v, top_groups) for h in range(count)]
        outgoing = rows[jnp.array(send)].reshape(len(send), share, count, top_rows)[:, :, jnp.array(order), :]
        outgoing = outgoing.reshape(len(send), share, count * top_rows)
        received = lax.ppermute(outgoing, "panel", [(i, i ^ v) for i in range(panels)])
        rows = rows[jnp.array(stay)] + received
        keep = [keep[i] for i in stay]
    total = rows[0]
    own_inverse = lax.dynamic_slice_in_dim(upper_inverse[0], begin, share, 1)
    own_base = jnp.einsum("kw,kr->wr", own_inverse, upper_rhs[0], precision=highest)

    top_held = xor_gather(top_solution, both, count, top_groups).reshape(count * top_rows, rhs)
    own_rows = own_base - jnp.einsum("wj,jr->wr", total, top_held, precision=highest)

    held = xor_gather(own_rows, both, count, spread_groups[:-1])
    last = spread_groups[-1][0]
    partner = lax.ppermute(held, both, [(i, i ^ (1 << last)) for i in range(count)])
    position = owner_map[parent_list]
    parent_rows = None
    for side, source in ((0, held), (1, partner)):
        offsets = jnp.array([o for o in range(panels) if ((o >> last) & 1) == side], jnp.int32)
        quarters = panel_index ^ offsets
        sources = position[:, None] * panels + quarters[None, :]
        places = xor_position(sources ^ me, spread_groups) - side * held.shape[0]
        slabs = source[places].reshape(position.shape[0], -1, own_rows.shape[1])
        within = lax.broadcasted_iota(jnp.int32, (offsets.shape[0], share), 1)
        columns = (quarters[:, None] * share + within).reshape(-1)
        pick = (lower_index[:, :, None] == columns[None, None, :]).astype(jnp.float32)
        term = jnp.einsum("skj,sjr->skr", pick, slabs, precision=highest)
        parent_rows = term if parent_rows is None else parent_rows + term

    panel_t = jnp.swapaxes(lower_panel, 1, 2)
    inverse_t = jnp.swapaxes(lower_inverse, 1, 2)
    lower_update = jnp.einsum("swk,skr->swr", panel_t, parent_rows, precision=highest)
    lower_solution = jnp.einsum(
        "swk,skr->swr", inverse_t, lower_rhs - lower_update, precision=highest
    )
    return (own_rows[None], lower_solution)


def solution(mesh):
    placed = (
        P("leaf", None, None),
        P("leaf", "panel", None),
        P("leaf", None, None),
        P("leaf", "panel"),
        P(("leaf", "panel"), None),
        P(),
        P(("leaf", "panel")),
        P(("leaf", "panel"), None),
        P(("leaf", "panel"), None, None),
        P(("leaf", "panel"), None, None),
        P(("leaf", "panel"), None, None),
    )
    return jax.shard_map(
        local,
        mesh=mesh,
        in_specs=placed,
        out_specs=(P("leaf", "panel", None), P(("leaf", "panel"), None, None)),
        check_vma=False,
    )
```

```python
import jax
import jax.numpy as jnp
from jax import lax
from jax.sharding import PartitionSpec as P


def xor_gather(block, axes, count, groups):
    held = block[None]
    for bits in groups:
        parts = [held]
        for k in range(1, 1 << len(bits)):
            v = sum(((k >> t) & 1) << b for t, b in enumerate(bits))
            parts.append(lax.ppermute(held, axes, [(i, i ^ v) for i in range(count)]))
        held = jnp.concatenate(parts, 0)
    return held


def xor_position(offset, groups):
    position = jnp.zeros_like(offset)
    stride = 1
    for bits in groups:
        k = sum(((offset >> b) & 1) << t for t, b in enumerate(bits))
        position = position + k * stride
        stride *= 1 << len(bits)
    return position


def xor_offset(position, groups):
    offset = jnp.zeros_like(position)
    stride = 1
    for bits in groups:
        k = (position // stride) % (1 << len(bits))
        for t, b in enumerate(bits):
            offset = offset | (((k >> t) & 1) << b)
        stride *= 1 << len(bits)
    return offset


def static_offset(position, groups):
    offset, stride = 0, 1
    for bits in groups:
        k = (position // stride) % (1 << len(bits))
        offset |= sum(((k >> t) & 1) << b for t, b in enumerate(bits))
        stride *= 1 << len(bits)
    return offset


def static_position(offset, groups):
    position, stride = 0, 1
    for bits in groups:
        position += sum(((offset >> b) & 1) << t for t, b in enumerate(bits)) * stride
        stride *= 1 << len(bits)
    return position


def log2(count):
    bits = count.bit_length() - 1
    assert (1 << bits) == count
    return bits


def local(
    upper_rhs,
    upper_panel,
    upper_inverse,
    top_index,
    top_solution,
    owner_map,
    parent_list,
    lower_index,
    lower_panel,
    lower_rhs,
    lower_inverse,
):
    highest = lax.Precision.HIGHEST
    leaves = lax.axis_size("leaf")
    panels = lax.axis_size("panel")
    count = leaves * panels
    both = ("leaf", "panel")
    me = lax.axis_index(both)
    panel_index = lax.axis_index("panel")
    width_upper = upper_rhs.shape[1]
    share = width_upper // panels
    begin = panel_index * share

    panel_bits = list(range(log2(panels)))
    leaf_bits = list(range(log2(panels), log2(count)))
    high_first = leaf_bits[::-1]
    leaf_groups = []
    if len(high_first) % 2:
        leaf_groups.append([high_first[0]])
        high_first = high_first[1:]
    leaf_groups += [high_first[i : i + 2] for i in range(0, len(high_first), 2)]
    top_groups = leaf_groups + [panel_bits]
    spread_groups = [[b] for b in panel_bits[1:]] + leaf_groups + [[0]]

    top_rows, rhs = top_solution.shape
    places = lax.broadcasted_iota(jnp.int32, (count, top_rows), 0)
    within = lax.broadcasted_iota(jnp.int32, (count, top_rows), 1)
    natural = ((me ^ xor_offset(places, top_groups)) * top_rows + within).reshape(-1)
    pick_top = (top_index[0][:, None] == natural[None, :]).astype(jnp.float32)
    folded = jnp.einsum("kv,vw->kw", upper_panel[0], upper_inverse[0], precision=highest)
    weights = jnp.einsum("kj,kw->wj", pick_top, folded, precision=highest)
    own_inverse = lax.dynamic_slice_in_dim(upper_inverse[0], begin, share, 1)
    own_base = jnp.einsum("kw,kr->wr", own_inverse, upper_rhs[0], precision=highest)

    top_held = xor_gather(top_solution, both, count, top_groups[:-1])
    top_size = top_held.size
    total = lax.dynamic_slice_in_dim(weights, begin, share, 0)
    parts = [top_held]
    for k in range(1, panels):
        v = sum(((k >> t) & 1) << b for t, b in enumerate(panel_bits))
        outgoing = lax.dynamic_slice_in_dim(weights, (panel_index ^ v) * share, share, 0)
        order = [static_position(static_offset(h, top_groups) ^ v, top_groups) for h in range(count)]
        outgoing = outgoing.reshape(share, count, top_rows)[:, jnp.array(order), :]
        message = jnp.concatenate([top_held.reshape(-1), outgoing.reshape(-1)])
        arrived = lax.ppermute(message, both, [(i, i ^ v) for i in range(count)])
        parts.append(arrived[:top_size].reshape(top_held.shape))
        total = total + arrived[top_size:].reshape(share, count * top_rows)
    top_held = jnp.concatenate(parts, 0).reshape(count * top_rows, rhs)
    own_rows = own_base - jnp.einsum("wj,jr->wr", total, top_held, precision=highest)

    held = xor_gather(own_rows, both, count, spread_groups[:-1])
    last = spread_groups[-1][0]
    partner = lax.ppermute(held, both, [(i, i ^ (1 << last)) for i in range(count)])
    position = owner_map[parent_list]
    parent_rows = None
    for side, source in ((0, held), (1, partner)):
        offsets = jnp.array([o for o in range(panels) if ((o >> last) & 1) == side], jnp.int32)
        quarters = panel_index ^ offsets
        sources = position[:, None] * panels + quarters[None, :]
        places = xor_position(sources ^ me, spread_groups) - side * held.shape[0]
        slabs = source[places].reshape(position.shape[0], -1, own_rows.shape[1])
        within = lax.broadcasted_iota(jnp.int32, (offsets.shape[0], share), 1)
        columns = (quarters[:, None] * share + within).reshape(-1)
        pick = (lower_index[:, :, None] == columns[None, None, :]).astype(jnp.float32)
        term = jnp.einsum("skj,sjr->skr", pick, slabs, precision=highest)
        parent_rows = term if parent_rows is None else parent_rows + term

    panel_t = jnp.swapaxes(lower_panel, 1, 2)
    inverse_t = jnp.swapaxes(lower_inverse, 1, 2)
    lower_update = jnp.einsum("swk,skr->swr", panel_t, parent_rows, precision=highest)
    lower_solution = jnp.einsum(
        "swk,skr->swr", inverse_t, lower_rhs - lower_update, precision=highest
    )
    return (own_rows[None], lower_solution)


def solution(mesh):
    placed = (
        P("leaf", None, None),
        P("leaf", "panel", None),
        P("leaf", None, None),
        P("leaf", "panel"),
        P(("leaf", "panel"), None),
        P(),
        P(("leaf", "panel")),
        P(("leaf", "panel"), None),
        P(("leaf", "panel"), None, None),
        P(("leaf", "panel"), None, None),
        P(("leaf", "panel"), None, None),
    )
    return jax.shard_map(
        local,
        mesh=mesh,
        in_specs=placed,
        out_specs=(P("leaf", "panel", None), P(("leaf", "panel"), None, None)),
        check_vma=False,
    )
```

```python
import jax
import jax.numpy as jnp
from jax import lax
from jax.sharding import PartitionSpec as P


def xor_gather(block, axes, count, groups):
    held = block[None]
    for bits in groups:
        parts = [held]
        for k in range(1, 1 << len(bits)):
            v = sum(((k >> t) & 1) << b for t, b in enumerate(bits))
            parts.append(lax.ppermute(held, axes, [(i, i ^ v) for i in range(count)]))
        held = jnp.concatenate(parts, 0)
    return held


def xor_position(offset, groups):
    position = jnp.zeros_like(offset)
    stride = 1
    for bits in groups:
        k = sum(((offset >> b) & 1) << t for t, b in enumerate(bits))
        position = position + k * stride
        stride *= 1 << len(bits)
    return position


def xor_offset(position, groups):
    offset = jnp.zeros_like(position)
    stride = 1
    for bits in groups:
        k = (position // stride) % (1 << len(bits))
        for t, b in enumerate(bits):
            offset = offset | (((k >> t) & 1) << b)
        stride *= 1 << len(bits)
    return offset


def static_offset(position, groups):
    offset, stride = 0, 1
    for bits in groups:
        k = (position // stride) % (1 << len(bits))
        offset |= sum(((k >> t) & 1) << b for t, b in enumerate(bits))
        stride *= 1 << len(bits)
    return offset


def static_position(offset, groups):
    position, stride = 0, 1
    for bits in groups:
        position += sum(((offset >> b) & 1) << t for t, b in enumerate(bits)) * stride
        stride *= 1 << len(bits)
    return position


def log2(count):
    bits = count.bit_length() - 1
    assert (1 << bits) == count
    return bits


def local(
    upper_rhs,
    upper_panel,
    upper_inverse,
    top_index,
    top_solution,
    owner_map,
    parent_list,
    lower_index,
    lower_panel,
    lower_rhs,
    lower_inverse,
):
    highest = lax.Precision.HIGHEST
    leaves = lax.axis_size("leaf")
    panels = lax.axis_size("panel")
    count = leaves * panels
    both = ("leaf", "panel")
    me = lax.axis_index(both)
    panel_index = lax.axis_index("panel")
    width_upper = upper_rhs.shape[1]
    share = width_upper // panels
    begin = panel_index * share

    panel_bits = list(range(log2(panels)))
    leaf_bits = list(range(log2(panels), log2(count)))
    high_first = leaf_bits[::-1]
    leaf_groups = []
    if len(high_first) % 2:
        leaf_groups.append([high_first[0]])
        high_first = high_first[1:]
    leaf_groups += [high_first[i : i + 2] for i in range(0, len(high_first), 2)]
    top_groups = [panel_bits] + leaf_groups
    spread_groups = [[b] for b in panel_bits[1:]] + leaf_groups + [[0]]

    top_rows, rhs = top_solution.shape
    places = lax.broadcasted_iota(jnp.int32, (count, top_rows), 0)
    within = lax.broadcasted_iota(jnp.int32, (count, top_rows), 1)
    natural = ((me ^ xor_offset(places, top_groups)) * top_rows + within).reshape(-1)
    pick_top = (top_index[0][:, None] == natural[None, :]).astype(jnp.float32)
    folded = jnp.einsum("kv,vw->kw", upper_panel[0], upper_inverse[0], precision=highest)
    weights = jnp.einsum("kj,kw->wj", pick_top, folded, precision=highest)
    total = lax.dynamic_slice_in_dim(weights, begin, share, 0)
    for v in range(1, panels):
        outgoing = lax.dynamic_slice_in_dim(weights, (panel_index ^ v) * share, share, 0)
        order = [static_position(static_offset(h, top_groups) ^ v, top_groups) for h in range(count)]
        outgoing = outgoing.reshape(share, count, top_rows)[:, jnp.array(order), :]
        outgoing = outgoing.reshape(share, count * top_rows)
        total = total + lax.ppermute(outgoing, "panel", [(i, i ^ v) for i in range(panels)])
    own_inverse = lax.dynamic_slice_in_dim(upper_inverse[0], begin, share, 1)
    own_base = jnp.einsum("kw,kr->wr", own_inverse, upper_rhs[0], precision=highest)

    top_held = xor_gather(top_solution, both, count, top_groups).reshape(count * top_rows, rhs)
    own_rows = own_base - jnp.einsum("wj,jr->wr", total, top_held, precision=highest)

    held = xor_gather(own_rows, both, count, spread_groups[:-1])
    last = spread_groups[-1][0]
    partner = lax.ppermute(held, both, [(i, i ^ (1 << last)) for i in range(count)])
    position = owner_map[parent_list]
    parent_rows = None
    for side, source in ((0, held), (1, partner)):
        offsets = jnp.array([o for o in range(panels) if ((o >> last) & 1) == side], jnp.int32)
        quarters = panel_index ^ offsets
        sources = position[:, None] * panels + quarters[None, :]
        places = xor_position(sources ^ me, spread_groups) - side * held.shape[0]
        slabs = source[places].reshape(position.shape[0], -1, own_rows.shape[1])
        within = lax.broadcasted_iota(jnp.int32, (offsets.shape[0], share), 1)
        columns = (quarters[:, None] * share + within).reshape(-1)
        pick = (lower_index[:, :, None] == columns[None, None, :]).astype(jnp.float32)
        term = jnp.einsum("skj,sjr->skr", pick, slabs, precision=highest)
        parent_rows = term if parent_rows is None else parent_rows + term

    panel_t = jnp.swapaxes(lower_panel, 1, 2)
    inverse_t = jnp.swapaxes(lower_inverse, 1, 2)
    lower_base = jnp.einsum("swk,skr->swr", inverse_t, lower_rhs, precision=highest)
    chained_t = jnp.einsum("swv,svk->swk", inverse_t, panel_t, precision=highest)
    lower_solution = lower_base - jnp.einsum("swk,skr->swr", chained_t, parent_rows, precision=highest)
    return (own_rows[None], lower_solution)


def solution(mesh):
    placed = (
        P("leaf", None, None),
        P("leaf", "panel", None),
        P("leaf", None, None),
        P("leaf", "panel"),
        P(("leaf", "panel"), None),
        P(),
        P(("leaf", "panel")),
        P(("leaf", "panel"), None),
        P(("leaf", "panel"), None, None),
        P(("leaf", "panel"), None, None),
        P(("leaf", "panel"), None, None),
    )
    return jax.shard_map(
        local,
        mesh=mesh,
        in_specs=placed,
        out_specs=(P("leaf", "panel", None), P(("leaf", "panel"), None, None)),
        check_vma=False,
    )
```

```python
import jax
import jax.numpy as jnp
from jax import lax
from jax.sharding import PartitionSpec as P


def xor_gather(block, axes, count, groups):
    held = block[None]
    for bits in groups:
        parts = [held]
        for k in range(1, 1 << len(bits)):
            v = sum(((k >> t) & 1) << b for t, b in enumerate(bits))
            parts.append(lax.ppermute(held, axes, [(i, i ^ v) for i in range(count)]))
        held = jnp.concatenate(parts, 0)
    return held


def xor_position(offset, groups):
    position = jnp.zeros_like(offset)
    stride = 1
    for bits in groups:
        k = sum(((offset >> b) & 1) << t for t, b in enumerate(bits))
        position = position + k * stride
        stride *= 1 << len(bits)
    return position


def xor_offset(position, groups):
    offset = jnp.zeros_like(position)
    stride = 1
    for bits in groups:
        k = (position // stride) % (1 << len(bits))
        for t, b in enumerate(bits):
            offset = offset | (((k >> t) & 1) << b)
        stride *= 1 << len(bits)
    return offset


def static_offset(position, groups):
    offset, stride = 0, 1
    for bits in groups:
        k = (position // stride) % (1 << len(bits))
        offset |= sum(((k >> t) & 1) << b for t, b in enumerate(bits))
        stride *= 1 << len(bits)
    return offset


def static_position(offset, groups):
    position, stride = 0, 1
    for bits in groups:
        position += sum(((offset >> b) & 1) << t for t, b in enumerate(bits)) * stride
        stride *= 1 << len(bits)
    return position


def log2(count):
    bits = count.bit_length() - 1
    assert (1 << bits) == count
    return bits


def local(
    upper_rhs,
    upper_panel,
    upper_inverse,
    top_index,
    top_solution,
    owner_map,
    parent_list,
    lower_index,
    lower_panel,
    lower_rhs,
    lower_inverse,
):
    highest = lax.Precision.HIGHEST
    leaves = lax.axis_size("leaf")
    panels = lax.axis_size("panel")
    count = leaves * panels
    both = ("leaf", "panel")
    me = lax.axis_index(both)
    panel_index = lax.axis_index("panel")
    width_upper = upper_rhs.shape[1]
    share = width_upper // panels
    begin = panel_index * share

    panel_bits = list(range(log2(panels)))
    leaf_bits = list(range(log2(panels), log2(count)))
    high_first = leaf_bits[::-1]
    leaf_groups = []
    if len(high_first) % 2:
        leaf_groups.append([high_first[0]])
        high_first = high_first[1:]
    leaf_groups += [high_first[i : i + 2] for i in range(0, len(high_first), 2)]
    top_groups = [panel_bits] + leaf_groups
    spread_groups = [[b] for b in panel_bits[1:]] + leaf_groups + [[0]]

    top_rows, rhs = top_solution.shape
    places = lax.broadcasted_iota(jnp.int32, (count, top_rows), 0)
    within = lax.broadcasted_iota(jnp.int32, (count, top_rows), 1)
    natural = ((me ^ xor_offset(places, top_groups)) * top_rows + within).reshape(-1)
    pick_top = (top_index[0][:, None] == natural[None, :]).astype(jnp.float32)
    folded = jnp.einsum("kv,vw->kw", upper_panel[0], upper_inverse[0], precision=highest)
    weights = jnp.einsum("kj,kw->wj", pick_top, folded, precision=highest)
    total = lax.dynamic_slice_in_dim(weights, begin, share, 0)
    for v in range(1, panels):
        outgoing = lax.dynamic_slice_in_dim(weights, (panel_index ^ v) * share, share, 0)
        order = [static_position(static_offset(h, top_groups) ^ v, top_groups) for h in range(count)]
        outgoing = outgoing.reshape(share, count, top_rows)[:, jnp.array(order), :]
        outgoing = outgoing.reshape(share, count * top_rows)
        total = total + lax.ppermute(outgoing, "panel", [(i, i ^ v) for i in range(panels)])
    own_inverse = lax.dynamic_slice_in_dim(upper_inverse[0], begin, share, 1)
    own_base = jnp.einsum("kw,kr->wr", own_inverse, upper_rhs[0], precision=highest)

    top_held = xor_gather(top_solution, both, count, top_groups).reshape(count * top_rows, rhs)
    own_rows = own_base - jnp.einsum("wj,jr->wr", total, top_held, precision=highest)

    held = xor_gather(own_rows, both, count, spread_groups[:-1])
    last = spread_groups[-1][0]
    partner = lax.ppermute(held, both, [(i, i ^ (1 << last)) for i in range(count)])
    position = owner_map[parent_list]
    parent_rows = None
    for side, source in ((0, held), (1, partner)):
        offsets = jnp.array([o for o in range(panels) if ((o >> last) & 1) == side], jnp.int32)
        quarters = panel_index ^ offsets
        sources = position[:, None] * panels + quarters[None, :]
        places = xor_position(sources ^ me, spread_groups) - side * held.shape[0]
        slabs = source[places].reshape(position.shape[0], -1, own_rows.shape[1])
        within = lax.broadcasted_iota(jnp.int32, (offsets.shape[0], share), 1)
        columns = (quarters[:, None] * share + within).reshape(-1)
        pick = (lower_index[:, :, None] == columns[None, None, :]).astype(jnp.float32)
        term = jnp.einsum("skj,sjr->skr", pick, slabs, precision=highest)
        if side == 0:
            partner, term = lax.optimization_barrier((partner, term))
        parent_rows = term if parent_rows is None else parent_rows + term

    panel_t = jnp.swapaxes(lower_panel, 1, 2)
    inverse_t = jnp.swapaxes(lower_inverse, 1, 2)
    lower_update = jnp.einsum("swk,skr->swr", panel_t, parent_rows, precision=highest)
    lower_solution = jnp.einsum(
        "swk,skr->swr", inverse_t, lower_rhs - lower_update, precision=highest
    )
    return (own_rows[None], lower_solution)


def solution(mesh):
    placed = (
        P("leaf", None, None),
        P("leaf", "panel", None),
        P("leaf", None, None),
        P("leaf", "panel"),
        P(("leaf", "panel"), None),
        P(),
        P(("leaf", "panel")),
        P(("leaf", "panel"), None),
        P(("leaf", "panel"), None, None),
        P(("leaf", "panel"), None, None),
        P(("leaf", "panel"), None, None),
    )
    return jax.shard_map(
        local,
        mesh=mesh,
        in_specs=placed,
        out_specs=(P("leaf", "panel", None), P(("leaf", "panel"), None, None)),
        check_vma=False,
    )
```

```python
import jax
import jax.numpy as jnp
from jax import lax
from jax.sharding import PartitionSpec as P


def xor_gather(block, axes, count, groups):
    held = block[None]
    for bits in groups:
        parts = [held]
        for k in range(1, 1 << len(bits)):
            v = sum(((k >> t) & 1) << b for t, b in enumerate(bits))
            parts.append(lax.ppermute(held, axes, [(i, i ^ v) for i in range(count)]))
        held = jnp.concatenate(parts, 0)
    return held


def xor_gather_step(held, axes, count, bits):
    parts = [held]
    for k in range(1, 1 << len(bits)):
        v = sum(((k >> t) & 1) << b for t, b in enumerate(bits))
        parts.append(lax.ppermute(held, axes, [(i, i ^ v) for i in range(count)]))
    return jnp.concatenate(parts, 0)


def xor_position(offset, groups):
    position = jnp.zeros_like(offset)
    stride = 1
    for bits in groups:
        k = sum(((offset >> b) & 1) << t for t, b in enumerate(bits))
        position = position + k * stride
        stride *= 1 << len(bits)
    return position


def xor_offset(position, groups):
    offset = jnp.zeros_like(position)
    stride = 1
    for bits in groups:
        k = (position // stride) % (1 << len(bits))
        for t, b in enumerate(bits):
            offset = offset | (((k >> t) & 1) << b)
        stride *= 1 << len(bits)
    return offset


def static_offset(position, groups):
    offset, stride = 0, 1
    for bits in groups:
        k = (position // stride) % (1 << len(bits))
        offset |= sum(((k >> t) & 1) << b for t, b in enumerate(bits))
        stride *= 1 << len(bits)
    return offset


def static_position(offset, groups):
    position, stride = 0, 1
    for bits in groups:
        position += sum(((offset >> b) & 1) << t for t, b in enumerate(bits)) * stride
        stride *= 1 << len(bits)
    return position


def log2(count):
    bits = count.bit_length() - 1
    assert (1 << bits) == count
    return bits


def local(
    upper_rhs,
    upper_panel,
    upper_inverse,
    top_index,
    top_solution,
    owner_map,
    parent_list,
    lower_index,
    lower_panel,
    lower_rhs,
    lower_inverse,
):
    highest = lax.Precision.HIGHEST
    leaves = lax.axis_size("leaf")
    panels = lax.axis_size("panel")
    count = leaves * panels
    both = ("leaf", "panel")
    me = lax.axis_index(both)
    panel_index = lax.axis_index("panel")
    width_upper = upper_rhs.shape[1]
    share = width_upper // panels
    begin = panel_index * share

    panel_bits = list(range(log2(panels)))
    leaf_bits = list(range(log2(panels), log2(count)))
    high_first = leaf_bits[::-1]
    leaf_groups = []
    if len(high_first) % 2:
        leaf_groups.append([high_first[0]])
        high_first = high_first[1:]
    leaf_groups += [high_first[i : i + 2] for i in range(0, len(high_first), 2)]
    top_groups = [panel_bits] + leaf_groups
    spread_groups = [[b] for b in panel_bits[1:]] + leaf_groups + [[0]]

    top_rows, rhs = top_solution.shape
    places = lax.broadcasted_iota(jnp.int32, (count, top_rows), 0)
    within = lax.broadcasted_iota(jnp.int32, (count, top_rows), 1)
    natural = ((me ^ xor_offset(places, top_groups)) * top_rows + within).reshape(-1)
    pick_top = (top_index[0][:, None] == natural[None, :]).astype(jnp.float32)
    folded = jnp.einsum("kv,vw->kw", upper_panel[0], upper_inverse[0], precision=highest)
    weights = jnp.einsum("kj,kw->wj", pick_top, folded, precision=highest)
    total = lax.dynamic_slice_in_dim(weights, begin, share, 0)
    for v in range(1, panels):
        outgoing = lax.dynamic_slice_in_dim(weights, (panel_index ^ v) * share, share, 0)
        order = [static_position(static_offset(h, top_groups) ^ v, top_groups) for h in range(count)]
        outgoing = outgoing.reshape(share, count, top_rows)[:, jnp.array(order), :]
        outgoing = outgoing.reshape(share, count * top_rows)
        total = total + lax.ppermute(outgoing, "panel", [(i, i ^ v) for i in range(panels)])
    own_inverse = lax.dynamic_slice_in_dim(upper_inverse[0], begin, share, 1)
    own_base = jnp.einsum("kw,kr->wr", own_inverse, upper_rhs[0], precision=highest)

    top_held = xor_gather(top_solution, both, count, top_groups).reshape(count * top_rows, rhs)
    own_rows = own_base - jnp.einsum("wj,jr->wr", total, top_held, precision=highest)

    inverse_t = jnp.swapaxes(lower_inverse, 1, 2)
    held = xor_gather_step(own_rows[None], both, count, spread_groups[0])
    _, inverse_late = lax.optimization_barrier((own_rows, lower_inverse))
    lower_base = jnp.einsum("skw,skr->swr", inverse_late, lower_rhs, precision=highest)
    held, lower_base = lax.optimization_barrier((held, lower_base))
    for bits in spread_groups[1:-1]:
        held = xor_gather_step(held, both, count, bits)
    last = spread_groups[-1][0]
    partner = lax.ppermute(held, both, [(i, i ^ (1 << last)) for i in range(count)])
    position = owner_map[parent_list]
    parent_rows = None
    for side, source in ((0, held), (1, partner)):
        offsets = jnp.array([o for o in range(panels) if ((o >> last) & 1) == side], jnp.int32)
        quarters = panel_index ^ offsets
        sources = position[:, None] * panels + quarters[None, :]
        places = xor_position(sources ^ me, spread_groups) - side * held.shape[0]
        slabs = source[places].reshape(position.shape[0], -1, own_rows.shape[1])
        within = lax.broadcasted_iota(jnp.int32, (offsets.shape[0], share), 1)
        columns = (quarters[:, None] * share + within).reshape(-1)
        pick = (lower_index[:, :, None] == columns[None, None, :]).astype(jnp.float32)
        term = jnp.einsum("skj,sjr->skr", pick, slabs, precision=highest)
        if side == 0:
            partner, term = lax.optimization_barrier((partner, term))
        parent_rows = term if parent_rows is None else parent_rows + term

    panel_t = jnp.swapaxes(lower_panel, 1, 2)
    lower_update = jnp.einsum("swk,skr->swr", panel_t, parent_rows, precision=highest)
    lower_solution = lower_base - jnp.einsum("swk,skr->swr", inverse_t, lower_update, precision=highest)
    return (own_rows[None], lower_solution)


def solution(mesh):
    placed = (
        P("leaf", None, None),
        P("leaf", "panel", None),
        P("leaf", None, None),
        P("leaf", "panel"),
        P(("leaf", "panel"), None),
        P(),
        P(("leaf", "panel")),
        P(("leaf", "panel"), None),
        P(("leaf", "panel"), None, None),
        P(("leaf", "panel"), None, None),
        P(("leaf", "panel"), None, None),
    )
    return jax.shard_map(
        local,
        mesh=mesh,
        in_specs=placed,
        out_specs=(P("leaf", "panel", None), P(("leaf", "panel"), None, None)),
        check_vma=False,
    )
```

```python
import jax
import jax.numpy as jnp
from jax import lax
from jax.sharding import PartitionSpec as P


def xor_gather(block, axes, count, groups):
    held = block[None]
    for bits in groups:
        parts = [held]
        for k in range(1, 1 << len(bits)):
            v = sum(((k >> t) & 1) << b for t, b in enumerate(bits))
            parts.append(lax.ppermute(held, axes, [(i, i ^ v) for i in range(count)]))
        held = jnp.concatenate(parts, 0)
    return held


def xor_position(offset, groups):
    position = jnp.zeros_like(offset)
    stride = 1
    for bits in groups:
        k = sum(((offset >> b) & 1) << t for t, b in enumerate(bits))
        position = position + k * stride
        stride *= 1 << len(bits)
    return position


def xor_offset(position, groups):
    offset = jnp.zeros_like(position)
    stride = 1
    for bits in groups:
        k = (position // stride) % (1 << len(bits))
        for t, b in enumerate(bits):
            offset = offset | (((k >> t) & 1) << b)
        stride *= 1 << len(bits)
    return offset


def static_offset(position, groups):
    offset, stride = 0, 1
    for bits in groups:
        k = (position // stride) % (1 << len(bits))
        offset |= sum(((k >> t) & 1) << b for t, b in enumerate(bits))
        stride *= 1 << len(bits)
    return offset


def static_position(offset, groups):
    position, stride = 0, 1
    for bits in groups:
        position += sum(((offset >> b) & 1) << t for t, b in enumerate(bits)) * stride
        stride *= 1 << len(bits)
    return position


def log2(count):
    bits = count.bit_length() - 1
    assert (1 << bits) == count
    return bits


def local(
    upper_rhs,
    upper_panel,
    upper_inverse,
    top_index,
    top_solution,
    owner_map,
    parent_list,
    lower_index,
    lower_panel,
    lower_rhs,
    lower_inverse,
):
    highest = lax.Precision.HIGHEST
    leaves = lax.axis_size("leaf")
    panels = lax.axis_size("panel")
    count = leaves * panels
    both = ("leaf", "panel")
    me = lax.axis_index(both)
    panel_index = lax.axis_index("panel")
    width_upper = upper_rhs.shape[1]
    share = width_upper // panels
    begin = panel_index * share

    panel_bits = list(range(log2(panels)))
    leaf_bits = list(range(log2(panels), log2(count)))
    high_first = leaf_bits[::-1]
    leaf_groups = []
    if len(high_first) % 2:
        leaf_groups.append([high_first[0]])
        high_first = high_first[1:]
    leaf_groups += [high_first[i : i + 2] for i in range(0, len(high_first), 2)]
    top_groups = [panel_bits] + leaf_groups
    spread_groups = [[b] for b in panel_bits[1:]] + leaf_groups + [[0]]

    top_rows, rhs = top_solution.shape
    places = lax.broadcasted_iota(jnp.int32, (count, top_rows), 0)
    within = lax.broadcasted_iota(jnp.int32, (count, top_rows), 1)
    natural = ((me ^ xor_offset(places, top_groups)) * top_rows + within).reshape(-1)
    pick_top = (top_index[0][:, None] == natural[None, :]).astype(jnp.float32)
    folded = jnp.einsum("kv,vw->kw", upper_panel[0], upper_inverse[0], precision=highest)
    weights = jnp.einsum("kj,kw->wj", pick_top, folded, precision=highest)
    total = lax.dynamic_slice_in_dim(weights, begin, share, 0)
    for v in range(1, panels):
        outgoing = lax.dynamic_slice_in_dim(weights, (panel_index ^ v) * share, share, 0)
        assert top_groups[0] == panel_bits
        width = len(panel_bits)
        outgoing = outgoing.reshape((share, count // panels) + (2,) * width + (top_rows,))
        flips = tuple(2 + width - 1 - t for t, b in enumerate(panel_bits) if (v >> b) & 1)
        outgoing = jnp.flip(outgoing, flips).reshape(share, count * top_rows)
        total = total + lax.ppermute(outgoing, "panel", [(i, i ^ v) for i in range(panels)])
    own_inverse = lax.dynamic_slice_in_dim(upper_inverse[0], begin, share, 1)
    own_base = jnp.einsum("kw,kr->wr", own_inverse, upper_rhs[0], precision=highest)

    top_held = xor_gather(top_solution, both, count, top_groups).reshape(count * top_rows, rhs)
    own_rows = own_base - jnp.einsum("wj,jr->wr", total, top_held, precision=highest)

    held = xor_gather(own_rows, both, count, spread_groups[:-1])
    last = spread_groups[-1][0]
    partner = lax.ppermute(held, both, [(i, i ^ (1 << last)) for i in range(count)])
    position = owner_map[parent_list]
    parent_rows = None
    for side, source in ((0, held), (1, partner)):
        offsets = jnp.array([o for o in range(panels) if ((o >> last) & 1) == side], jnp.int32)
        quarters = panel_index ^ offsets
        sources = position[:, None] * panels + quarters[None, :]
        places = xor_position(sources ^ me, spread_groups) - side * held.shape[0]
        slabs = source[places].reshape(position.shape[0], -1, own_rows.shape[1])
        within = lax.broadcasted_iota(jnp.int32, (offsets.shape[0], share), 1)
        columns = (quarters[:, None] * share + within).reshape(-1)
        pick = (lower_index[:, :, None] == columns[None, None, :]).astype(jnp.float32)
        term = jnp.einsum("skj,sjr->skr", pick, slabs, precision=highest)
        if side == 0:
            partner, term = lax.optimization_barrier((partner, term))
        parent_rows = term if parent_rows is None else parent_rows + term

    panel_t = jnp.swapaxes(lower_panel, 1, 2)
    inverse_t = jnp.swapaxes(lower_inverse, 1, 2)
    lower_update = jnp.einsum("swk,skr->swr", panel_t, parent_rows, precision=highest)
    lower_solution = jnp.einsum(
        "swk,skr->swr", inverse_t, lower_rhs - lower_update, precision=highest
    )
    return (own_rows[None], lower_solution)


def solution(mesh):
    placed = (
        P("leaf", None, None),
        P("leaf", "panel", None),
        P("leaf", None, None),
        P("leaf", "panel"),
        P(("leaf", "panel"), None),
        P(),
        P(("leaf", "panel")),
        P(("leaf", "panel"), None),
        P(("leaf", "panel"), None, None),
        P(("leaf", "panel"), None, None),
        P(("leaf", "panel"), None, None),
    )
    return jax.shard_map(
        local,
        mesh=mesh,
        in_specs=placed,
        out_specs=(P("leaf", "panel", None), P(("leaf", "panel"), None, None)),
        check_vma=False,
    )
```

```python
import jax
import jax.numpy as jnp
from jax import lax
from jax.sharding import PartitionSpec as P


def xor_gather(block, axes, count, groups):
    held = block[None]
    for bits in groups:
        parts = [held]
        for k in range(1, 1 << len(bits)):
            v = sum(((k >> t) & 1) << b for t, b in enumerate(bits))
            parts.append(lax.ppermute(held, axes, [(i, i ^ v) for i in range(count)]))
        held = jnp.concatenate(parts, 0)
    return held


def xor_position(offset, groups):
    position = jnp.zeros_like(offset)
    stride = 1
    for bits in groups:
        k = sum(((offset >> b) & 1) << t for t, b in enumerate(bits))
        position = position + k * stride
        stride *= 1 << len(bits)
    return position


def xor_offset(position, groups):
    offset = jnp.zeros_like(position)
    stride = 1
    for bits in groups:
        k = (position // stride) % (1 << len(bits))
        for t, b in enumerate(bits):
            offset = offset | (((k >> t) & 1) << b)
        stride *= 1 << len(bits)
    return offset


def static_offset(position, groups):
    offset, stride = 0, 1
    for bits in groups:
        k = (position // stride) % (1 << len(bits))
        offset |= sum(((k >> t) & 1) << b for t, b in enumerate(bits))
        stride *= 1 << len(bits)
    return offset


def static_position(offset, groups):
    position, stride = 0, 1
    for bits in groups:
        position += sum(((offset >> b) & 1) << t for t, b in enumerate(bits)) * stride
        stride *= 1 << len(bits)
    return position


def log2(count):
    bits = count.bit_length() - 1
    assert (1 << bits) == count
    return bits


def local(
    upper_rhs,
    upper_panel,
    upper_inverse,
    top_index,
    top_solution,
    owner_map,
    parent_list,
    lower_index,
    lower_panel,
    lower_rhs,
    lower_inverse,
):
    highest = lax.Precision.HIGHEST
    leaves = lax.axis_size("leaf")
    panels = lax.axis_size("panel")
    count = leaves * panels
    both = ("leaf", "panel")
    me = lax.axis_index(both)
    panel_index = lax.axis_index("panel")
    width_upper = upper_rhs.shape[1]
    share = width_upper // panels
    begin = panel_index * share

    panel_bits = list(range(log2(panels)))
    leaf_bits = list(range(log2(panels), log2(count)))
    high_first = leaf_bits[::-1]
    leaf_groups = []
    if len(high_first) % 2:
        leaf_groups.append([high_first[0]])
        high_first = high_first[1:]
    leaf_groups += [high_first[i : i + 2] for i in range(0, len(high_first), 2)]
    top_groups = [panel_bits] + leaf_groups
    spread_groups = [[b] for b in panel_bits[1:]] + leaf_groups + [[0]]

    top_rows, rhs = top_solution.shape
    places = lax.broadcasted_iota(jnp.int32, (count, top_rows), 0)
    within = lax.broadcasted_iota(jnp.int32, (count, top_rows), 1)
    natural = ((me ^ xor_offset(places, top_groups)) * top_rows + within).reshape(-1)
    pick_top = (top_index[0][:, None] == natural[None, :]).astype(jnp.float32)
    folded = jnp.einsum("kv,vw->kw", upper_panel[0], upper_inverse[0], precision=highest)
    weights = jnp.einsum("kj,kw->wj", pick_top, folded, precision=highest)
    total = lax.dynamic_slice_in_dim(weights, begin, share, 0)
    for v in range(1, panels):
        outgoing = lax.dynamic_slice_in_dim(weights, (panel_index ^ v) * share, share, 0)
        order = [static_position(static_offset(h, top_groups) ^ v, top_groups) for h in range(count)]
        outgoing = outgoing.reshape(share, count, top_rows)[:, jnp.array(order), :]
        outgoing = outgoing.reshape(share, count * top_rows)
        total = total + lax.ppermute(outgoing, "panel", [(i, i ^ v) for i in range(panels)])
    own_inverse = lax.dynamic_slice_in_dim(upper_inverse[0], begin, share, 1)
    own_base = jnp.einsum("kw,kr->wr", own_inverse, upper_rhs[0], precision=highest)

    top_held = xor_gather(top_solution, both, count, top_groups).reshape(count * top_rows, rhs)
    own_rows = own_base - jnp.einsum("wj,jr->wr", total, top_held, precision=highest)

    held = xor_gather(own_rows, both, count, spread_groups[:-1])
    last = spread_groups[-1][0]
    partner = lax.ppermute(held, both, [(i, i ^ (1 << last)) for i in range(count)])
    position = owner_map[parent_list]
    parent_rows = None
    for side, source in ((0, held), (1, partner)):
        offsets = jnp.array([o for o in range(panels) if ((o >> last) & 1) == side], jnp.int32)
        quarters = panel_index ^ offsets
        sources = position[:, None] * panels + quarters[None, :]
        places = xor_position(sources ^ me, spread_groups) - side * held.shape[0]
        slabs = source[places].reshape(position.shape[0], -1, own_rows.shape[1])
        within = lax.broadcasted_iota(jnp.int32, (offsets.shape[0], share), 1)
        columns = (quarters[:, None] * share + within).reshape(-1)
        pick = (lower_index[:, :, None] == columns[None, None, :]).astype(jnp.float32)
        term = jnp.einsum("skj,sjr->skr", pick, slabs, precision=highest)
        if side == 0:
            partner, term = lax.optimization_barrier((partner, term))
        parent_rows = term if parent_rows is None else parent_rows + term

    parent_rows = lax.optimization_barrier(parent_rows)
    panel_t = jnp.swapaxes(lower_panel, 1, 2)
    inverse_t = jnp.swapaxes(lower_inverse, 1, 2)
    lower_update = jnp.einsum("swk,skr->swr", panel_t, parent_rows, precision=highest)
    lower_solution = jnp.einsum(
        "swk,skr->swr", inverse_t, lower_rhs - lower_update, precision=highest
    )
    return (own_rows[None], lower_solution)


def solution(mesh):
    placed = (
        P("leaf", None, None),
        P("leaf", "panel", None),
        P("leaf", None, None),
        P("leaf", "panel"),
        P(("leaf", "panel"), None),
        P(),
        P(("leaf", "panel")),
        P(("leaf", "panel"), None),
        P(("leaf", "panel"), None, None),
        P(("leaf", "panel"), None, None),
        P(("leaf", "panel"), None, None),
    )
    return jax.shard_map(
        local,
        mesh=mesh,
        in_specs=placed,
        out_specs=(P("leaf", "panel", None), P(("leaf", "panel"), None, None)),
        check_vma=False,
    )
```

```python
import jax
import jax.numpy as jnp
from jax import lax
from jax.sharding import PartitionSpec as P


def xor_gather(block, axes, count, groups):
    held = block[None]
    for bits in groups:
        parts = [held]
        for k in range(1, 1 << len(bits)):
            v = sum(((k >> t) & 1) << b for t, b in enumerate(bits))
            parts.append(lax.ppermute(held, axes, [(i, i ^ v) for i in range(count)]))
        held = jnp.concatenate(parts, 0)
    return held


def xor_gather_step(held, axes, count, bits):
    parts = [held]
    for k in range(1, 1 << len(bits)):
        v = sum(((k >> t) & 1) << b for t, b in enumerate(bits))
        parts.append(lax.ppermute(held, axes, [(i, i ^ v) for i in range(count)]))
    return jnp.concatenate(parts, 0)


def xor_position(offset, groups):
    position = jnp.zeros_like(offset)
    stride = 1
    for bits in groups:
        k = sum(((offset >> b) & 1) << t for t, b in enumerate(bits))
        position = position + k * stride
        stride *= 1 << len(bits)
    return position


def xor_offset(position, groups):
    offset = jnp.zeros_like(position)
    stride = 1
    for bits in groups:
        k = (position // stride) % (1 << len(bits))
        for t, b in enumerate(bits):
            offset = offset | (((k >> t) & 1) << b)
        stride *= 1 << len(bits)
    return offset


def static_offset(position, groups):
    offset, stride = 0, 1
    for bits in groups:
        k = (position // stride) % (1 << len(bits))
        offset |= sum(((k >> t) & 1) << b for t, b in enumerate(bits))
        stride *= 1 << len(bits)
    return offset


def static_position(offset, groups):
    position, stride = 0, 1
    for bits in groups:
        position += sum(((offset >> b) & 1) << t for t, b in enumerate(bits)) * stride
        stride *= 1 << len(bits)
    return position


def log2(count):
    bits = count.bit_length() - 1
    assert (1 << bits) == count
    return bits


def local(
    upper_rhs,
    upper_panel,
    upper_inverse,
    top_index,
    top_solution,
    owner_map,
    parent_list,
    lower_index,
    lower_panel,
    lower_rhs,
    lower_inverse,
):
    highest = lax.Precision.HIGHEST
    leaves = lax.axis_size("leaf")
    panels = lax.axis_size("panel")
    count = leaves * panels
    both = ("leaf", "panel")
    me = lax.axis_index(both)
    panel_index = lax.axis_index("panel")
    width_upper = upper_rhs.shape[1]
    share = width_upper // panels
    begin = panel_index * share

    panel_bits = list(range(log2(panels)))
    leaf_bits = list(range(log2(panels), log2(count)))
    high_first = leaf_bits[::-1]
    leaf_groups = []
    if len(high_first) % 2:
        leaf_groups.append([high_first[0]])
        high_first = high_first[1:]
    leaf_groups += [high_first[i : i + 2] for i in range(0, len(high_first), 2)]
    top_groups = [panel_bits] + leaf_groups
    spread_groups = [[b] for b in panel_bits[1:]] + leaf_groups + [[0]]

    top_rows, rhs = top_solution.shape
    places = lax.broadcasted_iota(jnp.int32, (count, top_rows), 0)
    within = lax.broadcasted_iota(jnp.int32, (count, top_rows), 1)
    natural = ((me ^ xor_offset(places, top_groups)) * top_rows + within).reshape(-1)
    pick_top = (top_index[0][:, None] == natural[None, :]).astype(jnp.float32)
    folded = jnp.einsum("kv,vw->kw", upper_panel[0], upper_inverse[0], precision=highest)
    weights = jnp.einsum("kj,kw->wj", pick_top, folded, precision=highest)
    total = lax.dynamic_slice_in_dim(weights, begin, share, 0)
    top_first = xor_gather_step(top_solution[None], both, count, top_groups[0])
    top_first, weights = lax.optimization_barrier((top_first, weights))
    for v in range(1, panels):
        outgoing = lax.dynamic_slice_in_dim(weights, (panel_index ^ v) * share, share, 0)
        order = [static_position(static_offset(h, top_groups) ^ v, top_groups) for h in range(count)]
        outgoing = outgoing.reshape(share, count, top_rows)[:, jnp.array(order), :]
        outgoing = outgoing.reshape(share, count * top_rows)
        total = total + lax.ppermute(outgoing, "panel", [(i, i ^ v) for i in range(panels)])
    own_inverse = lax.dynamic_slice_in_dim(upper_inverse[0], begin, share, 1)
    own_base = jnp.einsum("kw,kr->wr", own_inverse, upper_rhs[0], precision=highest)

    top_held = top_first
    for bits in top_groups[1:]:
        top_held = xor_gather_step(top_held, both, count, bits)
    top_held = top_held.reshape(count * top_rows, rhs)
    own_rows = own_base - jnp.einsum("wj,jr->wr", total, top_held, precision=highest)

    held = xor_gather(own_rows, both, count, spread_groups[:-1])
    last = spread_groups[-1][0]
    partner = lax.ppermute(held, both, [(i, i ^ (1 << last)) for i in range(count)])
    position = owner_map[parent_list]
    parent_rows = None
    for side, source in ((0, held), (1, partner)):
        offsets = jnp.array([o for o in range(panels) if ((o >> last) & 1) == side], jnp.int32)
        quarters = panel_index ^ offsets
        sources = position[:, None] * panels + quarters[None, :]
        places = xor_position(sources ^ me, spread_groups) - side * held.shape[0]
        slabs = source[places].reshape(position.shape[0], -1, own_rows.shape[1])
        within = lax.broadcasted_iota(jnp.int32, (offsets.shape[0], share), 1)
        columns = (quarters[:, None] * share + within).reshape(-1)
        pick = (lower_index[:, :, None] == columns[None, None, :]).astype(jnp.float32)
        term = jnp.einsum("skj,sjr->skr", pick, slabs, precision=highest)
        if side == 0:
            partner, term = lax.optimization_barrier((partner, term))
        parent_rows = term if parent_rows is None else parent_rows + term

    panel_t = jnp.swapaxes(lower_panel, 1, 2)
    inverse_t = jnp.swapaxes(lower_inverse, 1, 2)
    lower_update = jnp.einsum("swk,skr->swr", panel_t, parent_rows, precision=highest)
    lower_solution = jnp.einsum(
        "swk,skr->swr", inverse_t, lower_rhs - lower_update, precision=highest
    )
    return (own_rows[None], lower_solution)


def solution(mesh):
    placed = (
        P("leaf", None, None),
        P("leaf", "panel", None),
        P("leaf", None, None),
        P("leaf", "panel"),
        P(("leaf", "panel"), None),
        P(),
        P(("leaf", "panel")),
        P(("leaf", "panel"), None),
        P(("leaf", "panel"), None, None),
        P(("leaf", "panel"), None, None),
        P(("leaf", "panel"), None, None),
    )
    return jax.shard_map(
        local,
        mesh=mesh,
        in_specs=placed,
        out_specs=(P("leaf", "panel", None), P(("leaf", "panel"), None, None)),
        check_vma=False,
    )
```

```python
import jax
import jax.numpy as jnp
from jax import lax
from jax.sharding import PartitionSpec as P


def xor_gather(block, axes, count, groups):
    held = block[None]
    for bits in groups:
        parts = [held]
        for k in range(1, 1 << len(bits)):
            v = sum(((k >> t) & 1) << b for t, b in enumerate(bits))
            parts.append(lax.ppermute(held, axes, [(i, i ^ v) for i in range(count)]))
        held = jnp.concatenate(parts, 0)
    return held


def xor_position(offset, groups):
    position = jnp.zeros_like(offset)
    stride = 1
    for bits in groups:
        k = sum(((offset >> b) & 1) << t for t, b in enumerate(bits))
        position = position + k * stride
        stride *= 1 << len(bits)
    return position


def xor_offset(position, groups):
    offset = jnp.zeros_like(position)
    stride = 1
    for bits in groups:
        k = (position // stride) % (1 << len(bits))
        for t, b in enumerate(bits):
            offset = offset | (((k >> t) & 1) << b)
        stride *= 1 << len(bits)
    return offset


def static_offset(position, groups):
    offset, stride = 0, 1
    for bits in groups:
        k = (position // stride) % (1 << len(bits))
        offset |= sum(((k >> t) & 1) << b for t, b in enumerate(bits))
        stride *= 1 << len(bits)
    return offset


def static_position(offset, groups):
    position, stride = 0, 1
    for bits in groups:
        position += sum(((offset >> b) & 1) << t for t, b in enumerate(bits)) * stride
        stride *= 1 << len(bits)
    return position


def log2(count):
    bits = count.bit_length() - 1
    assert (1 << bits) == count
    return bits


def local(
    upper_rhs,
    upper_panel,
    upper_inverse,
    top_index,
    top_solution,
    owner_map,
    parent_list,
    lower_index,
    lower_panel,
    lower_rhs,
    lower_inverse,
):
    highest = lax.Precision.HIGHEST
    leaves = lax.axis_size("leaf")
    panels = lax.axis_size("panel")
    count = leaves * panels
    both = ("leaf", "panel")
    me = lax.axis_index(both)
    panel_index = lax.axis_index("panel")
    width_upper = upper_rhs.shape[1]
    share = width_upper // panels
    begin = panel_index * share

    panel_bits = list(range(log2(panels)))
    leaf_bits = list(range(log2(panels), log2(count)))
    high_first = leaf_bits[::-1]
    leaf_groups = []
    if len(high_first) % 2:
        leaf_groups.append([high_first[0]])
        high_first = high_first[1:]
    leaf_groups += [high_first[i : i + 2] for i in range(0, len(high_first), 2)]
    top_groups = [panel_bits] + leaf_groups
    spread_groups = [[b] for b in panel_bits[1:]] + leaf_groups + [[0]]

    top_rows, rhs = top_solution.shape
    places = lax.broadcasted_iota(jnp.int32, (count, top_rows), 0)
    within = lax.broadcasted_iota(jnp.int32, (count, top_rows), 1)
    natural = ((me ^ xor_offset(places, top_groups)) * top_rows + within).reshape(-1)
    pick_top = (top_index[0][:, None] == natural[None, :]).astype(jnp.float32)
    folded = jnp.einsum("kv,vw->kw", upper_panel[0], upper_inverse[0], precision=highest)
    weights = jnp.einsum("kj,kw->wj", pick_top, folded, precision=highest)
    total = lax.dynamic_slice_in_dim(weights, begin, share, 0)
    for v in range(1, panels):
        outgoing = lax.dynamic_slice_in_dim(weights, (panel_index ^ v) * share, share, 0)
        order = [static_position(static_offset(h, top_groups) ^ v, top_groups) for h in range(count)]
        outgoing = outgoing.reshape(share, count, top_rows)[:, jnp.array(order), :]
        outgoing = outgoing.reshape(share, count * top_rows)
        total = total + lax.ppermute(outgoing, "panel", [(i, i ^ v) for i in range(panels)])
    own_inverse = lax.dynamic_slice_in_dim(upper_inverse[0], begin, share, 1)
    own_base = jnp.einsum("kw,kr->wr", own_inverse, upper_rhs[0], precision=highest)

    top_held = xor_gather(top_solution, both, count, top_groups[:-1])
    first = top_held.shape[0] * top_rows
    partial = own_base - jnp.einsum(
        "wj,jr->wr", total[:, :first], top_held.reshape(first, rhs), precision=highest
    )
    arrivals = []
    bits = top_groups[-1]
    for k in range(1, 1 << len(bits)):
        v = sum(((k >> t) & 1) << b for t, b in enumerate(bits))
        arrivals.append(lax.ppermute(top_held, both, [(i, i ^ v) for i in range(count)]))
    arrivals, partial = lax.optimization_barrier((arrivals, partial))
    own_rows = partial
    for k, block in enumerate(arrivals):
        columns = total[:, first * (k + 1) : first * (k + 2)]
        own_rows = own_rows - jnp.einsum("wj,jr->wr", columns, block.reshape(first, rhs), precision=highest)

    held = xor_gather(own_rows, both, count, spread_groups[:-1])
    last = spread_groups[-1][0]
    partner = lax.ppermute(held, both, [(i, i ^ (1 << last)) for i in range(count)])
    position = owner_map[parent_list]
    parent_rows = None
    for side, source in ((0, held), (1, partner)):
        offsets = jnp.array([o for o in range(panels) if ((o >> last) & 1) == side], jnp.int32)
        quarters = panel_index ^ offsets
        sources = position[:, None] * panels + quarters[None, :]
        places = xor_position(sources ^ me, spread_groups) - side * held.shape[0]
        slabs = source[places].reshape(position.shape[0], -1, own_rows.shape[1])
        within = lax.broadcasted_iota(jnp.int32, (offsets.shape[0], share), 1)
        columns = (quarters[:, None] * share + within).reshape(-1)
        pick = (lower_index[:, :, None] == columns[None, None, :]).astype(jnp.float32)
        term = jnp.einsum("skj,sjr->skr", pick, slabs, precision=highest)
        if side == 0:
            partner, term = lax.optimization_barrier((partner, term))
        parent_rows = term if parent_rows is None else parent_rows + term

    panel_t = jnp.swapaxes(lower_panel, 1, 2)
    inverse_t = jnp.swapaxes(lower_inverse, 1, 2)
    lower_update = jnp.einsum("swk,skr->swr", panel_t, parent_rows, precision=highest)
    lower_solution = jnp.einsum(
        "swk,skr->swr", inverse_t, lower_rhs - lower_update, precision=highest
    )
    return (own_rows[None], lower_solution)


def solution(mesh):
    placed = (
        P("leaf", None, None),
        P("leaf", "panel", None),
        P("leaf", None, None),
        P("leaf", "panel"),
        P(("leaf", "panel"), None),
        P(),
        P(("leaf", "panel")),
        P(("leaf", "panel"), None),
        P(("leaf", "panel"), None, None),
        P(("leaf", "panel"), None, None),
        P(("leaf", "panel"), None, None),
    )
    return jax.shard_map(
        local,
        mesh=mesh,
        in_specs=placed,
        out_specs=(P("leaf", "panel", None), P(("leaf", "panel"), None, None)),
        check_vma=False,
    )
```

```python
import jax
import jax.numpy as jnp
from jax import lax
from jax.sharding import PartitionSpec as P


def xor_gather(block, axes, count, groups):
    held = block[None]
    for bits in groups:
        parts = [held]
        for k in range(1, 1 << len(bits)):
            v = sum(((k >> t) & 1) << b for t, b in enumerate(bits))
            parts.append(lax.ppermute(held, axes, [(i, i ^ v) for i in range(count)]))
        held = jnp.concatenate(parts, 0)
    return held


def xor_position(offset, groups):
    position = jnp.zeros_like(offset)
    stride = 1
    for bits in groups:
        k = sum(((offset >> b) & 1) << t for t, b in enumerate(bits))
        position = position + k * stride
        stride *= 1 << len(bits)
    return position


def xor_offset(position, groups):
    offset = jnp.zeros_like(position)
    stride = 1
    for bits in groups:
        k = (position // stride) % (1 << len(bits))
        for t, b in enumerate(bits):
            offset = offset | (((k >> t) & 1) << b)
        stride *= 1 << len(bits)
    return offset


def static_offset(position, groups):
    offset, stride = 0, 1
    for bits in groups:
        k = (position // stride) % (1 << len(bits))
        offset |= sum(((k >> t) & 1) << b for t, b in enumerate(bits))
        stride *= 1 << len(bits)
    return offset


def static_position(offset, groups):
    position, stride = 0, 1
    for bits in groups:
        position += sum(((offset >> b) & 1) << t for t, b in enumerate(bits)) * stride
        stride *= 1 << len(bits)
    return position


def log2(count):
    bits = count.bit_length() - 1
    assert (1 << bits) == count
    return bits


def local(
    upper_rhs,
    upper_panel,
    upper_inverse,
    top_index,
    top_solution,
    owner_map,
    parent_list,
    lower_index,
    lower_panel,
    lower_rhs,
    lower_inverse,
):
    highest = lax.Precision.HIGHEST
    leaves = lax.axis_size("leaf")
    panels = lax.axis_size("panel")
    count = leaves * panels
    both = ("leaf", "panel")
    me = lax.axis_index(both)
    panel_index = lax.axis_index("panel")
    width_upper = upper_rhs.shape[1]
    share = width_upper // panels
    begin = panel_index * share

    panel_bits = list(range(log2(panels)))
    leaf_bits = list(range(log2(panels), log2(count)))
    high_first = leaf_bits[::-1]
    leaf_groups = []
    if len(high_first) % 2:
        leaf_groups.append([high_first[0]])
        high_first = high_first[1:]
    leaf_groups += [high_first[i : i + 2] for i in range(0, len(high_first), 2)]
    top_groups = [panel_bits] + leaf_groups[::-1]
    spread_groups = [[b] for b in panel_bits[1:]] + leaf_groups + [[0]]

    top_rows, rhs = top_solution.shape
    places = lax.broadcasted_iota(jnp.int32, (count, top_rows), 0)
    within = lax.broadcasted_iota(jnp.int32, (count, top_rows), 1)
    natural = ((me ^ xor_offset(places, top_groups)) * top_rows + within).reshape(-1)
    pick_top = (top_index[0][:, None] == natural[None, :]).astype(jnp.float32)
    folded = jnp.einsum("kv,vw->kw", upper_panel[0], upper_inverse[0], precision=highest)
    weights = jnp.einsum("kj,kw->wj", pick_top, folded, precision=highest)
    total = lax.dynamic_slice_in_dim(weights, begin, share, 0)
    for v in range(1, panels):
        outgoing = lax.dynamic_slice_in_dim(weights, (panel_index ^ v) * share, share, 0)
        order = [static_position(static_offset(h, top_groups) ^ v, top_groups) for h in range(count)]
        outgoing = outgoing.reshape(share, count, top_rows)[:, jnp.array(order), :]
        outgoing = outgoing.reshape(share, count * top_rows)
        total = total + lax.ppermute(outgoing, "panel", [(i, i ^ v) for i in range(panels)])
    own_inverse = lax.dynamic_slice_in_dim(upper_inverse[0], begin, share, 1)
    own_base = jnp.einsum("kw,kr->wr", own_inverse, upper_rhs[0], precision=highest)

    top_held = xor_gather(top_solution, both, count, top_groups).reshape(count * top_rows, rhs)
    own_rows = own_base - jnp.einsum("wj,jr->wr", total, top_held, precision=highest)

    held = xor_gather(own_rows, both, count, spread_groups[:-1])
    last = spread_groups[-1][0]
    partner = lax.ppermute(held, both, [(i, i ^ (1 << last)) for i in range(count)])
    position = owner_map[parent_list]
    parent_rows = None
    for side, source in ((0, held), (1, partner)):
        offsets = jnp.array([o for o in range(panels) if ((o >> last) & 1) == side], jnp.int32)
        quarters = panel_index ^ offsets
        sources = position[:, None] * panels + quarters[None, :]
        places = xor_position(sources ^ me, spread_groups) - side * held.shape[0]
        slabs = source[places].reshape(position.shape[0], -1, own_rows.shape[1])
        within = lax.broadcasted_iota(jnp.int32, (offsets.shape[0], share), 1)
        columns = (quarters[:, None] * share + within).reshape(-1)
        pick = (lower_index[:, :, None] == columns[None, None, :]).astype(jnp.float32)
        term = jnp.einsum("skj,sjr->skr", pick, slabs, precision=highest)
        if side == 0:
            partner, term = lax.optimization_barrier((partner, term))
        parent_rows = term if parent_rows is None else parent_rows + term

    panel_t = jnp.swapaxes(lower_panel, 1, 2)
    inverse_t = jnp.swapaxes(lower_inverse, 1, 2)
    lower_update = jnp.einsum("swk,skr->swr", panel_t, parent_rows, precision=highest)
    lower_solution = jnp.einsum(
        "swk,skr->swr", inverse_t, lower_rhs - lower_update, precision=highest
    )
    return (own_rows[None], lower_solution)


def solution(mesh):
    placed = (
        P("leaf", None, None),
        P("leaf", "panel", None),
        P("leaf", None, None),
        P("leaf", "panel"),
        P(("leaf", "panel"), None),
        P(),
        P(("leaf", "panel")),
        P(("leaf", "panel"), None),
        P(("leaf", "panel"), None, None),
        P(("leaf", "panel"), None, None),
        P(("leaf", "panel"), None, None),
    )
    return jax.shard_map(
        local,
        mesh=mesh,
        in_specs=placed,
        out_specs=(P("leaf", "panel", None), P(("leaf", "panel"), None, None)),
        check_vma=False,
    )
```
